256 devices in a mesh: ctx: 32 (over z, x), tp: 8 (over y, core).
Axes of the slice: x: 4, y: 4, z: 8, core: 2. Of those that a mesh axis runs over, the one named last changes fastest.
Arguments:
- activations: bfloat16 [8192, 4096], P('ctx'), may hold values from -38 to 38
- w_qkv: bfloat16 [4096, 6144], P(None, 'tp'), may hold values from -0.09375 to 0.09375
- matching: int32 [8, 32], P('tp'), may hold values from 0 to 31, each once within a row
- dropout_bits: int32 [8192, 512], P('ctx', 'tp'), may hold values from 0 to 65535
- out_grad: bfloat16 [8192, 2048], P('ctx', 'tp'), may hold values from -0.29882812 to 0.29882812
Outputs:
- attended: bfloat16 [8192, 2048], P('ctx', 'tp')
- input_grad: bfloat16 [8192, 4096], P('ctx', 'tp')
- weight_grad: bfloat16 [4096, 6144], P('ctx', 'tp')
The draws below stay inside these ranges and needn't reach their ends.
Inputs may be any that keep to these rules, and one draw needn't show every extreme that they name: Each row of matching is a permutation of the 32 blocks.
All inputs are finite; a program needn't handle non-finite values.
Results may differ from the reference program's by a relative error of at most 0.019.
Values may be sent and summed in bfloat16 or wider, within the bound.
No kernel may reach another device: no remote copies, remote signals or barrier semaphores. Data moves between devices by JAX's collectives and lax.ppermute only.
A program may use at most 128 MiB of HBM per device.

```python
import jax
import jax.numpy as jnp
from jax import lax

D = 4096
HEADS = 16
HD = 128
BLK = 256
HGROUP = 2
TOK_DEV = 256
WORDS = 32
TOKENS = 8192
NB = 32
GROUPS = 8
N_CTX = 32


def draw_activations(key, part):
    base = jnp.clip(jax.random.normal(jax.random.fold_in(key, 11), (TOKENS, D), jnp.float32), -5.0, 5.0)
    pairing = jax.random.permutation(jax.random.fold_in(key, 12), N_CTX)
    row_shard = jnp.arange(TOKENS) // TOK_DEV
    col_shard = jnp.arange(D) // (D // N_CTX)
    spiked = jnp.where(pairing[row_shard][:, None] == col_shard[None, :], 3.0, 1.0)
    return (base * spiked).astype(jnp.bfloat16)


def set_ends(array, stream_key, least, top_value):
    extent = array.shape
    index_at = [jax.random.randint(jax.random.fold_in(stream_key, axis), (), 0, extent[axis]) for axis in range(len(extent))]
    array = array.at[tuple(index_at)].set(least)
    longest = extent.index(max(extent))
    index_at[longest] = (index_at[longest] + 1) % extent[longest]
    return array.at[tuple(index_at)].set(top_value)


def shard_levels(own_key, dims, cuts, smallest, top_value):
    level = 1.0
    for position, blocks in cuts:
        heights = jax.random.uniform(jax.random.fold_in(jax.random.fold_in(own_key, 6), position), (blocks,), jnp.float32, smallest / len(cuts), top_value / len(cuts))
        level = level * jnp.repeat(jnp.exp(heights), dims[position] // blocks).reshape((-1,) + (1,) * (len(dims) - 1 - position))
    return level


def noise(rng, extent, deviation, most, split=(), kind=jnp.bfloat16):
    result = deviation * jax.random.normal(rng, extent, jnp.float32)
    if split:
        result = result * shard_levels(rng, extent, split, -0.22, 0.18)
    return jnp.clip(result, -most, most).astype(kind)


def setup_inputs(seed: int = 0) -> dict:
    seeds = jax.random.split(jax.random.key(seed), 6)
    activations = draw_activations(jax.random.fold_in(seeds[5], 71), 0)
    w_qkv = noise(seeds[1], (D, 3 * HEADS * HD), D ** -0.5, 0.09375, ((1, 8),))
    matching = jax.vmap(lambda own: jax.random.permutation(own, NB))(jax.random.split(seeds[2], GROUPS)).reshape((GROUPS, NB)).astype(jnp.int32)
    dropout_bits = set_ends(jax.random.randint(seeds[3], (TOKENS, HEADS * WORDS), 0, 65536), jax.random.fold_in(seeds[3], 1), 0, 65535).astype(jnp.int32)
    out_grad = noise(seeds[4], (TOKENS, HEADS * HD), 0.05, 0.29882812, ((0, 32), (1, 8)))
    return {"activations": activations, "w_qkv": w_qkv, "matching": matching, "dropout_bits": dropout_bits, "out_grad": out_grad}


def unpack_bits(words):
    shifts = jnp.arange(16, dtype=jnp.int32)
    bits = jnp.bitwise_and(jnp.right_shift(words[..., None], shifts), 1)
    return bits.reshape(words.shape[:-1] + (words.shape[-1] * 16,)).astype(jnp.float32) * 2.0


def to_blocks(flat, width):
    row_total = flat.shape[0]
    head_count = flat.shape[1] // width
    return flat.reshape(row_total // BLK, BLK, head_count, width).transpose(2, 0, 1, 3)


def from_blocks(blocked):
    head_count, block_count, block_rows, width = blocked.shape
    return blocked.transpose(1, 2, 0, 3).reshape(block_count * block_rows, head_count * width)


def mult(form, left, right):
    return jnp.einsum(form, left.astype(jnp.float32), right.astype(jnp.float32), precision=lax.Precision.HIGHEST)


def reference(activations, w_qkv, matching, dropout_bits, out_grad):
    score_scale = HD ** -0.5
    projected = jnp.dot(activations.astype(jnp.float32), w_qkv.astype(jnp.float32), precision=lax.Precision.HIGHEST).astype(jnp.bfloat16)
    projected = projected.reshape(TOKENS, HEADS, 3, HD)
    query = to_blocks(projected[:, :, 0].reshape(TOKENS, HEADS * HD), HD)
    key_own = to_blocks(projected[:, :, 1].reshape(TOKENS, HEADS * HD), HD)
    value_own = to_blocks(projected[:, :, 2].reshape(TOKENS, HEADS * HD), HD)
    head_match = matching[jnp.arange(HEADS) // HGROUP]
    head_index = jnp.arange(HEADS)[:, None]
    keys = jnp.concatenate([key_own, key_own[head_index, head_match]], 2)
    values = jnp.concatenate([value_own, value_own[head_index, head_match]], 2)
    scores = mult('hnqd,hnkd->hnqk', query, keys) * score_scale
    row_max = jnp.max(scores, -1, keepdims=True)
    log_total = row_max + jnp.log(jnp.sum(jnp.exp(scores - row_max), -1, keepdims=True))
    probability = jnp.exp(scores - log_total)
    kept = unpack_bits(to_blocks(dropout_bits, WORDS))
    dropped = (probability * kept).astype(jnp.bfloat16)
    attended = mult('hnqk,hnkd->hnqd', dropped, values).astype(jnp.bfloat16)
    grad_out = to_blocks(out_grad, HD)
    grad_prob = mult('hnqd,hnkd->hnqk', grad_out, values) * kept
    row_delta = jnp.sum(probability * grad_prob, -1, keepdims=True)
    grad_score = (probability * (grad_prob - row_delta) * score_scale).astype(jnp.bfloat16)
    grad_query = mult('hnqk,hnkd->hnqd', grad_score, keys).astype(jnp.bfloat16)
    grad_keys = mult('hnqk,hnqd->hnkd', grad_score, query)
    grad_values = mult('hnqk,hnqd->hnkd', dropped, grad_out)
    far_part = jnp.concatenate([grad_keys[:, :, BLK:], grad_values[:, :, BLK:]], -1)
    far_round = lax.optimization_barrier(far_part.astype(jnp.bfloat16)).astype(jnp.float32)
    placed = jnp.zeros_like(far_round).at[head_index, head_match].set(far_round)
    grad_key = (grad_keys[:, :, :BLK] + placed[..., :HD]).astype(jnp.bfloat16)
    grad_value = (grad_values[:, :, :BLK] + placed[..., HD:]).astype(jnp.bfloat16)
    stacked = jnp.stack([grad_query, grad_key, grad_value], 3)
    grad_qkv = stacked.transpose(1, 2, 0, 3, 4).reshape(TOKENS, 3 * HEADS * HD)
    input_grad = jnp.dot(grad_qkv.astype(jnp.float32), w_qkv.astype(jnp.float32).T, precision=lax.Precision.HIGHEST).astype(jnp.bfloat16)
    shard_inputs = activations.reshape(N_CTX, TOK_DEV, D)
    shard_grads = grad_qkv.reshape(N_CTX, TOK_DEV, 3 * HEADS * HD)

    def accumulate(running, pair):
        term = jnp.dot(pair[0].astype(jnp.float32).T, pair[1].astype(jnp.float32), precision=lax.Precision.HIGHEST)
        rounded = lax.optimization_barrier(term.astype(jnp.bfloat16))
        return running + rounded.astype(jnp.float32), None

    start_total = jnp.zeros((D, 3 * HEADS * HD), jnp.float32)
    weight_total, _ = lax.scan(accumulate, start_total, (shard_inputs, shard_grads))
    return from_blocks(attended), input_grad, weight_total.astype(jnp.bfloat16)
```

```python
import jax
import jax.numpy as jnp
import numpy as np
from jax import lax
from jax.sharding import Mesh, PartitionSpec as P

HD = 128
BLK = 256
HGROUP = 2
WORDS = 32


def unpack_bits(words):
    shifts = jnp.arange(16, dtype=jnp.int32)
    bits = jnp.bitwise_and(jnp.right_shift(words[..., None], shifts), 1)
    return bits.reshape(words.shape[:-1] + (words.shape[-1] * 16,)).astype(jnp.float32) * 2.0


def to_blocks(flat, width):
    row_total = flat.shape[0]
    head_count = flat.shape[1] // width
    return flat.reshape(row_total // BLK, BLK, head_count, width).transpose(2, 0, 1, 3)


def from_blocks(blocked):
    head_count, block_count, block_rows, width = blocked.shape
    return blocked.transpose(1, 2, 0, 3).reshape(block_count * block_rows, head_count * width)


CTX = ("z", "x")
TP = ("y", "c")


def route(payload, order):
    spread = lax.all_to_all(payload, CTX, 0, 0, tiled=True)
    chosen = jnp.take(spread, order, axis=0)
    return lax.all_to_all(chosen, CTX, 0, 0, tiled=True)


def to_pieces(blocked, pieces):
    lead = blocked.shape[:-2]
    rows, width = blocked.shape[-2:]
    split = blocked.reshape(lead + (pieces, rows // pieces, width))
    return jnp.moveaxis(split, len(lead), 0)


def from_pieces(spread):
    joined = jnp.moveaxis(spread, 0, -3)
    return joined.reshape(joined.shape[:-3] + (-1, joined.shape[-1]))


def ring_rs(chunks, axis, n):
    i = lax.axis_index(axis)
    if n == 2:
        other = lax.dynamic_index_in_dim(chunks, 1 - i, 0, keepdims=False)
        mine = lax.dynamic_index_in_dim(chunks, i, 0, keepdims=False)
        got = lax.ppermute(other, axis, [(0, 1), (1, 0)])
        return (got.astype(jnp.float32) + mine.astype(jnp.float32)).astype(chunks.dtype)
    half = chunks.shape[1] // 2
    cw = [(j, (j + 1) % n) for j in range(n)]
    ccw = [(j, (j - 1) % n) for j in range(n)]

    def take(k, part):
        block = lax.dynamic_index_in_dim(chunks, k % n, 0, keepdims=False)
        return block[:half] if part == 0 else block[half:]

    acc_a = take(i - 1 + n, 0)
    acc_b = take(i + 1, 1)
    for s in range(n - 1):
        got_a = lax.ppermute(acc_a, axis, cw)
        got_b = lax.ppermute(acc_b, axis, ccw)
        acc_a = (got_a.astype(jnp.float32) + take(i - s - 2 + 2 * n, 0).astype(jnp.float32)).astype(chunks.dtype)
        acc_b = (got_b.astype(jnp.float32) + take(i + s + 2, 1).astype(jnp.float32)).astype(chunks.dtype)
    return jnp.concatenate([acc_a, acc_b], 0)


def per_device(activations, w_qkv, matching, dropout_bits, out_grad):
    f32 = jnp.float32
    local_tokens = activations.shape[0]
    head_count = out_grad.shape[1] // HD
    score_scale = HD ** (-0.5)
    n_ctx = matching.shape[1]
    projected = jnp.dot(activations, w_qkv, preferred_element_type=f32).astype(jnp.bfloat16)
    projected = projected.reshape(local_tokens, head_count, 3, HD)
    query = to_blocks(projected[:, :, 0].reshape(local_tokens, head_count * HD), HD)
    key_own = to_blocks(projected[:, :, 1].reshape(local_tokens, head_count * HD), HD)
    value_own = to_blocks(projected[:, :, 2].reshape(local_tokens, head_count * HD), HD)
    order = matching[0]
    inverse = jnp.zeros_like(order).at[order].set(jnp.arange(n_ctx, dtype=order.dtype))
    own_kv = jnp.stack([key_own, value_own], 0)
    far_kv = from_pieces(route(to_pieces(own_kv, n_ctx), order))
    keys = jnp.concatenate([key_own, far_kv[0]], 2)
    values = jnp.concatenate([value_own, far_kv[1]], 2)
    scores = jnp.einsum("hnqd,hnkd->hnqk", query, keys, preferred_element_type=f32) * score_scale
    row_max = jnp.max(scores, -1, keepdims=True)
    log_total = row_max + jnp.log(jnp.sum(jnp.exp(scores - row_max), -1, keepdims=True))
    probability = jnp.exp(scores - log_total)
    kept = unpack_bits(to_blocks(dropout_bits, WORDS))
    dropped = (probability * kept).astype(jnp.bfloat16)
    attended = jnp.einsum("hnqk,hnkd->hnqd", dropped, values, preferred_element_type=f32).astype(
        jnp.bfloat16
    )
    grad_out = to_blocks(out_grad, HD)
    grad_prob = jnp.einsum("hnqd,hnkd->hnqk", grad_out, values, preferred_element_type=f32) * kept
    row_delta = jnp.sum(probability * grad_prob, -1, keepdims=True)
    grad_score = (probability * (grad_prob - row_delta) * score_scale).astype(jnp.bfloat16)
    grad_query = jnp.einsum("hnqk,hnkd->hnqd", grad_score, keys, preferred_element_type=f32).astype(
        jnp.bfloat16
    )
    grad_keys = jnp.einsum("hnqk,hnqd->hnkd", grad_score, query, preferred_element_type=f32)
    grad_values = jnp.einsum("hnqk,hnqd->hnkd", dropped, grad_out, preferred_element_type=f32)
    far_part = jnp.stack([grad_keys[:, :, BLK:], grad_values[:, :, BLK:]], 0).astype(jnp.bfloat16)
    returned = from_pieces(route(to_pieces(far_part, n_ctx), inverse))
    grad_key = (grad_keys[:, :, :BLK] + returned[0].astype(f32)).astype(jnp.bfloat16)
    grad_value = (grad_values[:, :, :BLK] + returned[1].astype(f32)).astype(jnp.bfloat16)
    stacked = jnp.stack([grad_query, grad_key, grad_value], 3)
    grad_qkv = stacked.transpose(1, 2, 0, 3, 4).reshape(local_tokens, head_count * 3 * HD)
    weight_part = lax.dot_general(
        activations, grad_qkv, (((0,), (0,)), ((), ())), preferred_element_type=f32
    ).astype(jnp.bfloat16)
    weight_grad = lax.psum_scatter(
        lax.psum_scatter(weight_part, "z", scatter_dimension=0, tiled=True),
        "x",
        scatter_dimension=0,
        tiled=True,
    )
    input_part = jnp.dot(grad_qkv, w_qkv.T, preferred_element_type=f32).astype(jnp.bfloat16)
    n_y = lax.psum(1, "y")
    width = input_part.shape[1] // (2 * n_y)
    by_core = input_part.reshape(local_tokens, n_y, 2, width).transpose(2, 1, 0, 3)
    core_sum = ring_rs(by_core, "c", 2)
    input_grad = ring_rs(core_sum, "y", n_y)
    return (from_blocks(attended), input_grad, weight_grad)


def solution(mesh):
    n_ctx, n_tp = mesh.devices.shape
    n_x = 4 if n_ctx % 4 == 0 else 1
    fine = Mesh(mesh.devices.reshape(n_ctx // n_x, n_x, n_tp // 2, 2), ("z", "x", "y", "c"))
    return jax.shard_map(
        per_device,
        mesh=fine,
        in_specs=(P(CTX, None), P(None, TP), P(TP, None), P(CTX, TP), P(CTX, TP)),
        out_specs=(P(CTX, TP), P(CTX, TP), P(CTX, TP)),
        check_vma=False,
    )
```

```python
import jax
import jax.numpy as jnp
import numpy as np
from jax import lax
from jax.sharding import Mesh, PartitionSpec as P

HD = 128
BLK = 256
HGROUP = 2
WORDS = 32


def unpack_bits(words):
    shifts = jnp.arange(16, dtype=jnp.int32)
    bits = jnp.bitwise_and(jnp.right_shift(words[..., None], shifts), 1)
    return bits.reshape(words.shape[:-1] + (words.shape[-1] * 16,)).astype(jnp.float32) * 2.0


def to_blocks(flat, width):
    row_total = flat.shape[0]
    head_count = flat.shape[1] // width
    return flat.reshape(row_total // BLK, BLK, head_count, width).transpose(2, 0, 1, 3)


def from_blocks(blocked):
    head_count, block_count, block_rows, width = blocked.shape
    return blocked.transpose(1, 2, 0, 3).reshape(block_count * block_rows, head_count * width)


CTX = ("z", "x")
TP = ("y", "c")


def route(payload, order):
    spread = lax.all_to_all(payload, CTX, 0, 0, tiled=True)
    chosen = jnp.take(spread, order, axis=0)
    return lax.all_to_all(chosen, CTX, 0, 0, tiled=True)


def to_pieces(blocked, pieces):
    lead = blocked.shape[:-2]
    rows, width = blocked.shape[-2:]
    split = blocked.reshape(lead + (pieces, rows // pieces, width))
    return jnp.moveaxis(split, len(lead), 0)


def from_pieces(spread):
    joined = jnp.moveaxis(spread, 0, -3)
    return joined.reshape(joined.shape[:-3] + (-1, joined.shape[-1]))


def ring_rs(chunks, axis, n):
    i = lax.axis_index(axis)
    if n == 2:
        other = lax.dynamic_index_in_dim(chunks, 1 - i, 0, keepdims=False)
        mine = lax.dynamic_index_in_dim(chunks, i, 0, keepdims=False)
        got = lax.ppermute(other, axis, [(0, 1), (1, 0)])
        return (got.astype(jnp.float32) + mine.astype(jnp.float32)).astype(chunks.dtype)
    half = chunks.shape[1] // 2
    cw = [(j, (j + 1) % n) for j in range(n)]
    ccw = [(j, (j - 1) % n) for j in range(n)]

    def take(k, part):
        block = lax.dynamic_index_in_dim(chunks, k % n, 0, keepdims=False)
        return block[:half] if part == 0 else block[half:]

    acc_a = take(i - 1 + n, 0)
    acc_b = take(i + 1, 1)
    for s in range(n - 1):
        got_a = lax.ppermute(acc_a, axis, cw)
        got_b = lax.ppermute(acc_b, axis, ccw)
        acc_a = (got_a.astype(jnp.float32) + take(i - s - 2 + 2 * n, 0).astype(jnp.float32)).astype(chunks.dtype)
        acc_b = (got_b.astype(jnp.float32) + take(i + s + 2, 1).astype(jnp.float32)).astype(chunks.dtype)
    return jnp.concatenate([acc_a, acc_b], 0)


def weight_term(activations, cols):
    return lax.dot_general(
        activations, cols, (((0,), (0,)), ((), ())), preferred_element_type=jnp.float32
    ).astype(jnp.bfloat16)


def reduce_ctx(part):
    part = lax.psum_scatter(part, "z", scatter_dimension=0, tiled=True)
    return lax.psum_scatter(part, "x", scatter_dimension=0, tiled=True)


def per_device(activations, w_qkv, matching, dropout_bits, out_grad):
    f32 = jnp.float32
    local_tokens = activations.shape[0]
    head_count = out_grad.shape[1] // HD
    score_scale = HD ** (-0.5)
    n_ctx = matching.shape[1]
    projected = jnp.dot(activations, w_qkv, preferred_element_type=f32).astype(jnp.bfloat16)
    projected = projected.reshape(local_tokens, head_count, 3, HD)
    query = to_blocks(projected[:, :, 0].reshape(local_tokens, head_count * HD), HD)
    key_own = to_blocks(projected[:, :, 1].reshape(local_tokens, head_count * HD), HD)
    value_own = to_blocks(projected[:, :, 2].reshape(local_tokens, head_count * HD), HD)
    order = matching[0]
    inverse = jnp.zeros_like(order).at[order].set(jnp.arange(n_ctx, dtype=order.dtype))
    own_kv = jnp.stack([key_own, value_own], 0)
    far_kv = from_pieces(route(to_pieces(own_kv, n_ctx), order))
    keys = jnp.concatenate([key_own, far_kv[0]], 2)
    values = jnp.concatenate([value_own, far_kv[1]], 2)
    scores = jnp.einsum("hnqd,hnkd->hnqk", query, keys, preferred_element_type=f32) * score_scale
    row_max = jnp.max(scores, -1, keepdims=True)
    log_total = row_max + jnp.log(jnp.sum(jnp.exp(scores - row_max), -1, keepdims=True))
    probability = jnp.exp(scores - log_total)
    kept = unpack_bits(to_blocks(dropout_bits, WORDS))
    dropped = (probability * kept).astype(jnp.bfloat16)
    attended = jnp.einsum("hnqk,hnkd->hnqd", dropped, values, preferred_element_type=f32).astype(
        jnp.bfloat16
    )
    grad_out = to_blocks(out_grad, HD)
    grad_prob = jnp.einsum("hnqd,hnkd->hnqk", grad_out, values, preferred_element_type=f32) * kept
    row_delta = jnp.sum(probability * grad_prob, -1, keepdims=True)
    grad_score = (probability * (grad_prob - row_delta) * score_scale).astype(jnp.bfloat16)
    grad_query = jnp.einsum("hnqk,hnkd->hnqd", grad_score, keys, preferred_element_type=f32).astype(
        jnp.bfloat16
    )
    grad_keys = jnp.einsum("hnqk,hnqd->hnkd", grad_score, query, preferred_element_type=f32)
    grad_values = jnp.einsum("hnqk,hnqd->hnkd", dropped, grad_out, preferred_element_type=f32)
    far_part = jnp.stack([grad_keys[:, :, BLK:], grad_values[:, :, BLK:]], 0).astype(jnp.bfloat16)
    returned = from_pieces(route(to_pieces(far_part, n_ctx), inverse))
    grad_key = (grad_keys[:, :, :BLK] + returned[0].astype(f32)).astype(jnp.bfloat16)
    grad_value = (grad_values[:, :, :BLK] + returned[1].astype(f32)).astype(jnp.bfloat16)
    stacked = jnp.stack([grad_query, grad_key, grad_value], 3)
    grad_qkv = stacked.transpose(1, 2, 0, 3, 4).reshape(local_tokens, head_count * 3 * HD)
    query_cols = grad_query.transpose(1, 2, 0, 3).reshape(local_tokens, head_count * HD)
    kv_cols = jnp.stack([grad_key, grad_value], 3).transpose(1, 2, 0, 3, 4)
    kv_cols = kv_cols.reshape(local_tokens, head_count * 2 * HD)
    weight_q = reduce_ctx(weight_term(activations, query_cols))
    weight_kv = reduce_ctx(weight_term(activations, kv_cols))
    rows = weight_q.shape[0]
    weight_grad = jnp.concatenate(
        [weight_q.reshape(rows, head_count, 1, HD), weight_kv.reshape(rows, head_count, 2, HD)], 2
    ).reshape(rows, head_count * 3 * HD)
    n_y = lax.psum(1, "y")
    width = activations.shape[1] // (2 * n_y)
    w_split = w_qkv.reshape(n_y, 2, width, w_qkv.shape[1])
    by_core = jnp.einsum("tk,ycwk->cytw", grad_qkv, w_split, preferred_element_type=f32)
    core_sum = ring_rs(by_core.astype(jnp.bfloat16), "c", 2)
    input_grad = ring_rs(core_sum, "y", n_y)
    return (from_blocks(attended), input_grad, weight_grad)


def solution(mesh):
    n_ctx, n_tp = mesh.devices.shape
    n_x = 4 if n_ctx % 4 == 0 else 1
    fine = Mesh(mesh.devices.reshape(n_ctx // n_x, n_x, n_tp // 2, 2), ("z", "x", "y", "c"))
    return jax.shard_map(
        per_device,
        mesh=fine,
        in_specs=(P(CTX, None), P(None, TP), P(TP, None), P(CTX, TP), P(CTX, TP)),
        out_specs=(P(CTX, TP), P(CTX, TP), P(CTX, TP)),
        check_vma=False,
    )
```

```python
import jax
import jax.numpy as jnp
import numpy as np
from jax import lax
from jax.sharding import Mesh, PartitionSpec as P

HD = 128
BLK = 256
HGROUP = 2
WORDS = 32


def unpack_bits(words):
    shifts = jnp.arange(16, dtype=jnp.int32)
    bits = jnp.bitwise_and(jnp.right_shift(words[..., None], shifts), 1)
    return bits.reshape(words.shape[:-1] + (words.shape[-1] * 16,)).astype(jnp.float32) * 2.0


def to_blocks(flat, width):
    row_total = flat.shape[0]
    head_count = flat.shape[1] // width
    return flat.reshape(row_total // BLK, BLK, head_count, width).transpose(2, 0, 1, 3)


def from_blocks(blocked):
    head_count, block_count, block_rows, width = blocked.shape
    return blocked.transpose(1, 2, 0, 3).reshape(block_count * block_rows, head_count * width)


CTX = ("z", "x")
TP = ("y", "c")


def route(payload, order):
    spread = lax.all_to_all(payload, CTX, 0, 0, tiled=True)
    chosen = jnp.take(spread, order, axis=0)
    return lax.all_to_all(chosen, CTX, 0, 0, tiled=True)


def to_pieces(blocked, pieces):
    lead = blocked.shape[:-2]
    rows, width = blocked.shape[-2:]
    split = blocked.reshape(lead + (pieces, rows // pieces, width))
    return jnp.moveaxis(split, len(lead), 0)


def from_pieces(spread):
    joined = jnp.moveaxis(spread, 0, -3)
    return joined.reshape(joined.shape[:-3] + (-1, joined.shape[-1]))


def ring_rs(chunks, axis, n):
    i = lax.axis_index(axis)
    if n == 2:
        other = lax.dynamic_index_in_dim(chunks, 1 - i, 0, keepdims=False)
        mine = lax.dynamic_index_in_dim(chunks, i, 0, keepdims=False)
        got = lax.ppermute(other, axis, [(0, 1), (1, 0)])
        return (got.astype(jnp.float32) + mine.astype(jnp.float32)).astype(chunks.dtype)
    half = chunks.shape[1] // 2
    cw = [(j, (j + 1) % n) for j in range(n)]
    ccw = [(j, (j - 1) % n) for j in range(n)]

    def take(k, part):
        block = lax.dynamic_index_in_dim(chunks, k % n, 0, keepdims=False)
        return block[:half] if part == 0 else block[half:]

    acc_a = take(i - 1 + n, 0)
    acc_b = take(i + 1, 1)
    for s in range(n - 1):
        got_a = lax.ppermute(acc_a, axis, cw)
        got_b = lax.ppermute(acc_b, axis, ccw)
        acc_a = (got_a.astype(jnp.float32) + take(i - s - 2 + 2 * n, 0).astype(jnp.float32)).astype(chunks.dtype)
        acc_b = (got_b.astype(jnp.float32) + take(i + s + 2, 1).astype(jnp.float32)).astype(chunks.dtype)
    return jnp.concatenate([acc_a, acc_b], 0)


def weight_term(activations, cols):
    return lax.dot_general(
        activations, cols, (((0,), (0,)), ((), ())), preferred_element_type=jnp.float32
    ).astype(jnp.bfloat16)


def reduce_ctx(part):
    part = lax.psum_scatter(part, "z", scatter_dimension=0, tiled=True)
    n_x = lax.psum(1, "x")
    pieces = part.reshape((n_x, part.shape[0] // n_x) + part.shape[1:])
    gathered = lax.all_to_all(pieces, "x", 0, 0, tiled=True)
    return jnp.sum(gathered.astype(jnp.float32), 0).astype(part.dtype)


def per_device(activations, w_qkv, matching, dropout_bits, out_grad):
    f32 = jnp.float32
    local_tokens = activations.shape[0]
    head_count = out_grad.shape[1] // HD
    score_scale = HD ** (-0.5)
    n_ctx = matching.shape[1]
    projected = jnp.dot(activations, w_qkv, preferred_element_type=f32).astype(jnp.bfloat16)
    projected = projected.reshape(local_tokens, head_count, 3, HD)
    query = to_blocks(projected[:, :, 0].reshape(local_tokens, head_count * HD), HD)
    key_own = to_blocks(projected[:, :, 1].reshape(local_tokens, head_count * HD), HD)
    value_own = to_blocks(projected[:, :, 2].reshape(local_tokens, head_count * HD), HD)
    order = matching[0]
    inverse = jnp.zeros_like(order).at[order].set(jnp.arange(n_ctx, dtype=order.dtype))
    own_kv = jnp.stack([key_own, value_own], 0)
    far_kv = from_pieces(route(to_pieces(own_kv, n_ctx), order))
    keys = jnp.concatenate([key_own, far_kv[0]], 2)
    values = jnp.concatenate([value_own, far_kv[1]], 2)
    scores = jnp.einsum("hnqd,hnkd->hnqk", query, keys, preferred_element_type=f32) * score_scale
    row_max = jnp.max(scores, -1, keepdims=True)
    log_total = row_max + jnp.log(jnp.sum(jnp.exp(scores - row_max), -1, keepdims=True))
    probability = jnp.exp(scores - log_total)
    kept = unpack_bits(to_blocks(dropout_bits, WORDS))
    dropped = (probability * kept).astype(jnp.bfloat16)
    attended = jnp.einsum("hnqk,hnkd->hnqd", dropped, values, preferred_element_type=f32).astype(
        jnp.bfloat16
    )
    grad_out = to_blocks(out_grad, HD)
    grad_prob = jnp.einsum("hnqd,hnkd->hnqk", grad_out, values, preferred_element_type=f32) * kept
    row_delta = jnp.sum(probability * grad_prob, -1, keepdims=True)
    grad_score = (probability * (grad_prob - row_delta) * score_scale).astype(jnp.bfloat16)
    grad_query = jnp.einsum("hnqk,hnkd->hnqd", grad_score, keys, preferred_element_type=f32).astype(
        jnp.bfloat16
    )
    grad_keys = jnp.einsum("hnqk,hnqd->hnkd", grad_score, query, preferred_element_type=f32)
    grad_values = jnp.einsum("hnqk,hnqd->hnkd", dropped, grad_out, preferred_element_type=f32)
    far_part = jnp.stack([grad_keys[:, :, BLK:], grad_values[:, :, BLK:]], 0).astype(jnp.bfloat16)
    returned = from_pieces(route(to_pieces(far_part, n_ctx), inverse))
    grad_key = (grad_keys[:, :, :BLK] + returned[0].astype(f32)).astype(jnp.bfloat16)
    grad_value = (grad_values[:, :, :BLK] + returned[1].astype(f32)).astype(jnp.bfloat16)
    stacked = jnp.stack([grad_query, grad_key, grad_value], 3)
    grad_qkv = stacked.transpose(1, 2, 0, 3, 4).reshape(local_tokens, head_count * 3 * HD)
    weight_grad = reduce_ctx(weight_term(activations, grad_qkv))
    n_y = lax.psum(1, "y")
    width = activations.shape[1] // (2 * n_y)
    w_split = w_qkv.reshape(n_y, 2, width, w_qkv.shape[1])
    by_core = jnp.einsum("tk,ycwk->cytw", grad_qkv, w_split, preferred_element_type=f32)
    core_sum = ring_rs(by_core.astype(jnp.bfloat16), "c", 2)
    input_grad = ring_rs(core_sum, "y", n_y)
    return (from_blocks(attended), input_grad, weight_grad)


def solution(mesh):
    n_ctx, n_tp = mesh.devices.shape
    n_x = 4 if n_ctx % 4 == 0 else 1
    fine = Mesh(mesh.devices.reshape(n_ctx // n_x, n_x, n_tp // 2, 2), ("z", "x", "y", "c"))
    return jax.shard_map(
        per_device,
        mesh=fine,
        in_specs=(P(CTX, None), P(None, TP), P(TP, None), P(CTX, TP), P(CTX, TP)),
        out_specs=(P(CTX, TP), P(CTX, TP), P(CTX, TP)),
        check_vma=False,
    )
```

```python
import jax
import jax.numpy as jnp
import numpy as np
from jax import lax
from jax.sharding import Mesh, PartitionSpec as P

HD = 128
BLK = 256
HGROUP = 2
WORDS = 32


def unpack_bits(words):
    shifts = jnp.arange(16, dtype=jnp.int32)
    bits = jnp.bitwise_and(jnp.right_shift(words[..., None], shifts), 1)
    return bits.reshape(words.shape[:-1] + (words.shape[-1] * 16,)).astype(jnp.float32) * 2.0


def to_blocks(flat, width):
    row_total = flat.shape[0]
    head_count = flat.shape[1] // width
    return flat.reshape(row_total // BLK, BLK, head_count, width).transpose(2, 0, 1, 3)


def from_blocks(blocked):
    head_count, block_count, block_rows, width = blocked.shape
    return blocked.transpose(1, 2, 0, 3).reshape(block_count * block_rows, head_count * width)


CTX = ("z", "x")
TP = ("y", "c")


def route(payload, order):
    spread = lax.all_to_all(payload, CTX, 0, 0, tiled=True)
    chosen = jnp.take(spread, order, axis=0)
    return lax.all_to_all(chosen, CTX, 0, 0, tiled=True)


def to_pieces(blocked, pieces):
    lead = blocked.shape[:-2]
    rows, width = blocked.shape[-2:]
    split = blocked.reshape(lead + (pieces, rows // pieces, width))
    return jnp.moveaxis(split, len(lead), 0)


def from_pieces(spread):
    joined = jnp.moveaxis(spread, 0, -3)
    return joined.reshape(joined.shape[:-3] + (-1, joined.shape[-1]))


def ring_rs(chunks, axis, n):
    i = lax.axis_index(axis)
    if n == 2:
        other = lax.dynamic_index_in_dim(chunks, 1 - i, 0, keepdims=False)
        mine = lax.dynamic_index_in_dim(chunks, i, 0, keepdims=False)
        got = lax.ppermute(other, axis, [(0, 1), (1, 0)])
        return (got.astype(jnp.float32) + mine.astype(jnp.float32)).astype(chunks.dtype)
    half = chunks.shape[1] // 2
    cw = [(j, (j + 1) % n) for j in range(n)]
    ccw = [(j, (j - 1) % n) for j in range(n)]

    def take(k, part):
        block = lax.dynamic_index_in_dim(chunks, k % n, 0, keepdims=False)
        return block[:half] if part == 0 else block[half:]

    acc_a = take(i - 1 + n, 0)
    acc_b = take(i + 1, 1)
    for s in range(n - 1):
        got_a = lax.ppermute(acc_a, axis, cw)
        got_b = lax.ppermute(acc_b, axis, ccw)
        acc_a = (got_a.astype(jnp.float32) + take(i - s - 2 + 2 * n, 0).astype(jnp.float32)).astype(chunks.dtype)
        acc_b = (got_b.astype(jnp.float32) + take(i + s + 2, 1).astype(jnp.float32)).astype(chunks.dtype)
    return jnp.concatenate([acc_a, acc_b], 0)


def weight_term(activations, cols):
    return lax.dot_general(
        activations, cols, (((0,), (0,)), ((), ())), preferred_element_type=jnp.float32
    ).astype(jnp.bfloat16)


def reduce_ctx(part):
    part = lax.psum_scatter(part, "z", scatter_dimension=0, tiled=True)
    n_x = lax.psum(1, "x")
    pieces = part.reshape((n_x, part.shape[0] // n_x) + part.shape[1:])
    gathered = lax.all_to_all(pieces, "x", 0, 0, tiled=True)
    return jnp.sum(gathered.astype(jnp.float32), 0).astype(part.dtype)


def reduce_ctx_x_first(part):
    n_x = lax.psum(1, "x")
    n_z = lax.psum(1, "z")
    rows = part.shape[0] // (n_x * n_z)
    pieces = part.reshape(n_z, n_x, rows, part.shape[1]).transpose(1, 0, 2, 3)
    gathered = lax.all_to_all(pieces, "x", 0, 0, tiled=True)
    summed = jnp.sum(gathered.astype(jnp.float32), 0).astype(part.dtype)
    return ring_rs(summed, "z", n_z)


def per_device(activations, w_qkv, matching, dropout_bits, out_grad):
    f32 = jnp.float32
    local_tokens = activations.shape[0]
    head_count = out_grad.shape[1] // HD
    score_scale = HD ** (-0.5)
    n_ctx = matching.shape[1]
    projected = jnp.dot(activations, w_qkv, preferred_element_type=f32).astype(jnp.bfloat16)
    projected = projected.reshape(local_tokens, head_count, 3, HD)
    query = to_blocks(projected[:, :, 0].reshape(local_tokens, head_count * HD), HD)
    key_own = to_blocks(projected[:, :, 1].reshape(local_tokens, head_count * HD), HD)
    value_own = to_blocks(projected[:, :, 2].reshape(local_tokens, head_count * HD), HD)
    order = matching[0]
    inverse = jnp.zeros_like(order).at[order].set(jnp.arange(n_ctx, dtype=order.dtype))
    own_kv = jnp.stack([key_own, value_own], 0)
    far_kv = from_pieces(route(to_pieces(own_kv, n_ctx), order))
    keys = jnp.concatenate([key_own, far_kv[0]], 2)
    values = jnp.concatenate([value_own, far_kv[1]], 2)
    scores = jnp.einsum("hnqd,hnkd->hnqk", query, keys, preferred_element_type=f32) * score_scale
    row_max = jnp.max(scores, -1, keepdims=True)
    log_total = row_max + jnp.log(jnp.sum(jnp.exp(scores - row_max), -1, keepdims=True))
    probability = jnp.exp(scores - log_total)
    kept = unpack_bits(to_blocks(dropout_bits, WORDS))
    dropped = (probability * kept).astype(jnp.bfloat16)
    attended = jnp.einsum("hnqk,hnkd->hnqd", dropped, values, preferred_element_type=f32).astype(
        jnp.bfloat16
    )
    grad_out = to_blocks(out_grad, HD)
    grad_prob = jnp.einsum("hnqd,hnkd->hnqk", grad_out, values, preferred_element_type=f32) * kept
    row_delta = jnp.sum(probability * grad_prob, -1, keepdims=True)
    grad_score = (probability * (grad_prob - row_delta) * score_scale).astype(jnp.bfloat16)
    grad_query = jnp.einsum("hnqk,hnkd->hnqd", grad_score, keys, preferred_element_type=f32).astype(
        jnp.bfloat16
    )
    grad_keys = jnp.einsum("hnqk,hnqd->hnkd", grad_score, query, preferred_element_type=f32)
    grad_values = jnp.einsum("hnqk,hnqd->hnkd", dropped, grad_out, preferred_element_type=f32)
    far_part = jnp.stack([grad_keys[:, :, BLK:], grad_values[:, :, BLK:]], 0).astype(jnp.bfloat16)
    returned = from_pieces(route(to_pieces(far_part, n_ctx), inverse))
    grad_key = (grad_keys[:, :, :BLK] + returned[0].astype(f32)).astype(jnp.bfloat16)
    grad_value = (grad_values[:, :, :BLK] + returned[1].astype(f32)).astype(jnp.bfloat16)
    stacked = jnp.stack([grad_query, grad_key, grad_value], 3)
    grad_qkv = stacked.transpose(1, 2, 0, 3, 4).reshape(local_tokens, head_count * 3 * HD)
    weight_part = weight_term(activations, grad_qkv)
    split = weight_part.shape[1] // 2
    weight_grad = jnp.concatenate(
        [reduce_ctx(weight_part[:, :split]), reduce_ctx_x_first(weight_part[:, split:])], 1
    )
    n_y = lax.psum(1, "y")
    width = activations.shape[1] // (2 * n_y)
    w_split = w_qkv.reshape(n_y, 2, width, w_qkv.shape[1])
    by_core = jnp.einsum("tk,ycwk->cytw", grad_qkv, w_split, preferred_element_type=f32)
    core_sum = ring_rs(by_core.astype(jnp.bfloat16), "c", 2)
    input_grad = ring_rs(core_sum, "y", n_y)
    return (from_blocks(attended), input_grad, weight_grad)


def solution(mesh):
    n_ctx, n_tp = mesh.devices.shape
    n_x = 4 if n_ctx % 4 == 0 else 1
    fine = Mesh(mesh.devices.reshape(n_ctx // n_x, n_x, n_tp // 2, 2), ("z", "x", "y", "c"))
    return jax.shard_map(
        per_device,
        mesh=fine,
        in_specs=(P(CTX, None), P(None, TP), P(TP, None), P(CTX, TP), P(CTX, TP)),
        out_specs=(P(CTX, TP), P(CTX, TP), P(CTX, TP)),
        check_vma=False,
    )
```

```python
import jax
import jax.numpy as jnp
import numpy as np
from jax import lax
from jax.sharding import Mesh, PartitionSpec as P

HD = 128
BLK = 256
HGROUP = 2
WORDS = 32


def unpack_bits(words):
    shifts = jnp.arange(16, dtype=jnp.int32)
    bits = jnp.bitwise_and(jnp.right_shift(words[..., None], shifts), 1)
    return bits.reshape(words.shape[:-1] + (words.shape[-1] * 16,)).astype(jnp.float32) * 2.0


def to_blocks(flat, width):
    row_total = flat.shape[0]
    head_count = flat.shape[1] // width
    return flat.reshape(row_total // BLK, BLK, head_count, width).transpose(2, 0, 1, 3)


def from_blocks(blocked):
    head_count, block_count, block_rows, width = blocked.shape
    return blocked.transpose(1, 2, 0, 3).reshape(block_count * block_rows, head_count * width)


CTX = ("z", "x")
TP = ("y", "c")


def route(payload, order):
    spread = lax.all_to_all(payload, CTX, 0, 0, tiled=True)
    pieces = spread.shape[0]
    pick = (order[:, None] == jnp.arange(pieces, dtype=order.dtype)[None, :]).astype(spread.dtype)
    flat = spread.reshape(pieces, -1)
    chosen = jnp.dot(pick, flat, preferred_element_type=jnp.float32).astype(spread.dtype)
    return lax.all_to_all(chosen.reshape(spread.shape), CTX, 0, 0, tiled=True)


def to_pieces(blocked, pieces):
    lead = blocked.shape[:-2]
    rows, width = blocked.shape[-2:]
    split = blocked.reshape(lead + (pieces, rows // pieces, width))
    return jnp.moveaxis(split, len(lead), 0)


def from_pieces(spread):
    joined = jnp.moveaxis(spread, 0, -3)
    return joined.reshape(joined.shape[:-3] + (-1, joined.shape[-1]))


def ring_rs(chunks, axis, n):
    i = lax.axis_index(axis)
    if n == 2:
        other = lax.dynamic_index_in_dim(chunks, 1 - i, 0, keepdims=False)
        mine = lax.dynamic_index_in_dim(chunks, i, 0, keepdims=False)
        got = lax.ppermute(other, axis, [(0, 1), (1, 0)])
        return (got.astype(jnp.float32) + mine.astype(jnp.float32)).astype(chunks.dtype)
    half = chunks.shape[1] // 2
    cw = [(j, (j + 1) % n) for j in range(n)]
    ccw = [(j, (j - 1) % n) for j in range(n)]

    def take(k, part):
        block = lax.dynamic_index_in_dim(chunks, k % n, 0, keepdims=False)
        return block[:half] if part == 0 else block[half:]

    acc_a = take(i - 1 + n, 0)
    acc_b = take(i + 1, 1)
    for s in range(n - 1):
        got_a = lax.ppermute(acc_a, axis, cw)
        got_b = lax.ppermute(acc_b, axis, ccw)
        acc_a = (got_a.astype(jnp.float32) + take(i - s - 2 + 2 * n, 0).astype(jnp.float32)).astype(chunks.dtype)
        acc_b = (got_b.astype(jnp.float32) + take(i + s + 2, 1).astype(jnp.float32)).astype(chunks.dtype)
    return jnp.concatenate([acc_a, acc_b], 0)


def weight_term(activations, cols):
    return lax.dot_general(
        activations, cols, (((0,), (0,)), ((), ())), preferred_element_type=jnp.float32
    ).astype(jnp.bfloat16)


def reduce_ctx(part):
    part = lax.psum_scatter(part, "z", scatter_dimension=0, tiled=True)
    n_x = lax.psum(1, "x")
    pieces = part.reshape((n_x, part.shape[0] // n_x) + part.shape[1:])
    gathered = lax.all_to_all(pieces, "x", 0, 0, tiled=True)
    return jnp.sum(gathered.astype(jnp.float32), 0).astype(part.dtype)


def per_device(activations, w_qkv, matching, dropout_bits, out_grad):
    f32 = jnp.float32
    local_tokens = activations.shape[0]
    head_count = out_grad.shape[1] // HD
    score_scale = HD ** (-0.5)
    n_ctx = matching.shape[1]
    projected = jnp.dot(activations, w_qkv, preferred_element_type=f32).astype(jnp.bfloat16)
    projected = projected.reshape(local_tokens, head_count, 3, HD)
    query = to_blocks(projected[:, :, 0].reshape(local_tokens, head_count * HD), HD)
    key_own = to_blocks(projected[:, :, 1].reshape(local_tokens, head_count * HD), HD)
    value_own = to_blocks(projected[:, :, 2].reshape(local_tokens, head_count * HD), HD)
    order = matching[0]
    inverse = jnp.zeros_like(order).at[order].set(jnp.arange(n_ctx, dtype=order.dtype))
    own_kv = jnp.stack([key_own, value_own], 0)
    far_kv = from_pieces(route(to_pieces(own_kv, n_ctx), order))
    key_far, value_far = far_kv[0], far_kv[1]

    def mm(form, left, right):
        return jnp.einsum(form, left, right, preferred_element_type=f32)

    score_own = mm("hnqd,hnkd->hnqk", query, key_own) * score_scale
    score_far = mm("hnqd,hnkd->hnqk", query, key_far) * score_scale
    row_max = jnp.maximum(jnp.max(score_own, -1, keepdims=True), jnp.max(score_far, -1, keepdims=True))
    total = jnp.sum(jnp.exp(score_own - row_max), -1, keepdims=True) + jnp.sum(
        jnp.exp(score_far - row_max), -1, keepdims=True
    )
    log_total = row_max + jnp.log(total)
    prob_own = jnp.exp(score_own - log_total)
    prob_far = jnp.exp(score_far - log_total)
    words = to_blocks(dropout_bits, WORDS)
    half_words = WORDS // 2
    kept_own = unpack_bits(words[..., :half_words])
    kept_far = unpack_bits(words[..., half_words:])
    dropped_own = (prob_own * kept_own).astype(jnp.bfloat16)
    dropped_far = (prob_far * kept_far).astype(jnp.bfloat16)
    attended = (
        mm("hnqk,hnkd->hnqd", dropped_own, value_own) + mm("hnqk,hnkd->hnqd", dropped_far, value_far)
    ).astype(jnp.bfloat16)
    grad_out = to_blocks(out_grad, HD)
    grad_prob_own = mm("hnqd,hnkd->hnqk", grad_out, value_own) * kept_own
    grad_prob_far = mm("hnqd,hnkd->hnqk", grad_out, value_far) * kept_far
    row_delta = jnp.sum(prob_own * grad_prob_own, -1, keepdims=True) + jnp.sum(
        prob_far * grad_prob_far, -1, keepdims=True
    )
    score_grad_own = (prob_own * (grad_prob_own - row_delta) * score_scale).astype(jnp.bfloat16)
    score_grad_far = (prob_far * (grad_prob_far - row_delta) * score_scale).astype(jnp.bfloat16)
    grad_query = (
        mm("hnqk,hnkd->hnqd", score_grad_own, key_own) + mm("hnqk,hnkd->hnqd", score_grad_far, key_far)
    ).astype(jnp.bfloat16)
    grad_key_own = mm("hnqk,hnqd->hnkd", score_grad_own, query)
    grad_value_own = mm("hnqk,hnqd->hnkd", dropped_own, grad_out)
    far_part = jnp.stack(
        [mm("hnqk,hnqd->hnkd", score_grad_far, query), mm("hnqk,hnqd->hnkd", dropped_far, grad_out)], 0
    ).astype(jnp.bfloat16)
    returned = from_pieces(route(to_pieces(far_part, n_ctx), inverse))
    grad_key = (grad_key_own + returned[0].astype(f32)).astype(jnp.bfloat16)
    grad_value = (grad_value_own + returned[1].astype(f32)).astype(jnp.bfloat16)
    stacked = jnp.stack([grad_query, grad_key, grad_value], 3)
    grad_qkv = stacked.transpose(1, 2, 0, 3, 4).reshape(local_tokens, head_count * 3 * HD)
    weight_grad = reduce_ctx(weight_term(activations, grad_qkv))
    n_y = lax.psum(1, "y")
    width = activations.shape[1] // (2 * n_y)
    w_split = w_qkv.reshape(n_y, 2, width, w_qkv.shape[1])
    by_core = jnp.einsum("tk,ycwk->cytw", grad_qkv, w_split, preferred_element_type=f32)
    core_sum = ring_rs(by_core.astype(jnp.bfloat16), "c", 2)
    input_grad = ring_rs(core_sum, "y", n_y)
    return (from_blocks(attended), input_grad, weight_grad)


def solution(mesh):
    n_ctx, n_tp = mesh.devices.shape
    n_x = 4 if n_ctx % 4 == 0 else 1
    fine = Mesh(mesh.devices.reshape(n_ctx // n_x, n_x, n_tp // 2, 2), ("z", "x", "y", "c"))
    return jax.shard_map(
        per_device,
        mesh=fine,
        in_specs=(P(CTX, None), P(None, TP), P(TP, None), P(CTX, TP), P(CTX, TP)),
        out_specs=(P(CTX, TP), P(CTX, TP), P(CTX, TP)),
        check_vma=False,
    )
```

```python
import jax
import jax.numpy as jnp
import numpy as np
from jax import lax
from jax.sharding import Mesh, PartitionSpec as P

HD = 128
BLK = 256
HGROUP = 2
WORDS = 32


def unpack_bits(words):
    shifts = jnp.arange(16, dtype=jnp.int32)
    bits = jnp.bitwise_and(jnp.right_shift(words[..., None], shifts), 1)
    return bits.reshape(words.shape[:-1] + (words.shape[-1] * 16,)).astype(jnp.float32) * 2.0


def to_blocks(flat, width):
    row_total = flat.shape[0]
    head_count = flat.shape[1] // width
    return flat.reshape(row_total // BLK, BLK, head_count, width).transpose(2, 0, 1, 3)


def from_blocks(blocked):
    head_count, block_count, block_rows, width = blocked.shape
    return blocked.transpose(1, 2, 0, 3).reshape(block_count * block_rows, head_count * width)


CTX = ("z", "x")
TP = ("y", "c")


def route(payload, order):
    spread = lax.all_to_all(payload, CTX, 0, 0, tiled=True)
    pieces = spread.shape[0]
    pick = (order[:, None] == jnp.arange(pieces, dtype=order.dtype)[None, :]).astype(spread.dtype)
    flat = spread.reshape(pieces, -1)
    chosen = jnp.dot(pick, flat, preferred_element_type=jnp.float32).astype(spread.dtype)
    return lax.all_to_all(chosen.reshape(spread.shape), CTX, 0, 0, tiled=True)


def to_pieces(blocked, pieces):
    lead = blocked.shape[:-2]
    rows, width = blocked.shape[-2:]
    split = blocked.reshape(lead + (pieces, rows // pieces, width))
    return jnp.moveaxis(split, len(lead), 0)


def from_pieces(spread):
    joined = jnp.moveaxis(spread, 0, -3)
    return joined.reshape(joined.shape[:-3] + (-1, joined.shape[-1]))


def ring_rs(chunks, axis, n):
    i = lax.axis_index(axis)
    if n == 2:
        other = lax.dynamic_index_in_dim(chunks, 1 - i, 0, keepdims=False)
        mine = lax.dynamic_index_in_dim(chunks, i, 0, keepdims=False)
        got = lax.ppermute(other, axis, [(0, 1), (1, 0)])
        return (got.astype(jnp.float32) + mine.astype(jnp.float32)).astype(chunks.dtype)
    half = chunks.shape[1] // 2
    cw = [(j, (j + 1) % n) for j in range(n)]
    ccw = [(j, (j - 1) % n) for j in range(n)]

    def take(k, part):
        block = lax.dynamic_index_in_dim(chunks, k % n, 0, keepdims=False)
        return block[:half] if part == 0 else block[half:]

    acc_a = take(i - 1 + n, 0)
    acc_b = take(i + 1, 1)
    for s in range(n - 1):
        got_a = lax.ppermute(acc_a, axis, cw)
        got_b = lax.ppermute(acc_b, axis, ccw)
        acc_a = (got_a.astype(jnp.float32) + take(i - s - 2 + 2 * n, 0).astype(jnp.float32)).astype(chunks.dtype)
        acc_b = (got_b.astype(jnp.float32) + take(i + s + 2, 1).astype(jnp.float32)).astype(chunks.dtype)
    return jnp.concatenate([acc_a, acc_b], 0)


def weight_term(activations, cols):
    return lax.dot_general(
        activations, cols, (((0,), (0,)), ((), ())), preferred_element_type=jnp.float32
    ).astype(jnp.bfloat16)


def reduce_ctx(part):
    part = lax.psum_scatter(part, "z", scatter_dimension=0, tiled=True)
    n_x = lax.psum(1, "x")
    pieces = part.reshape((n_x, part.shape[0] // n_x) + part.shape[1:])
    gathered = lax.all_to_all(pieces, "x", 0, 0, tiled=True)
    return jnp.sum(gathered.astype(jnp.float32), 0).astype(part.dtype)


def per_device(activations, w_qkv, matching, dropout_bits, out_grad):
    f32 = jnp.float32
    local_tokens = activations.shape[0]
    head_count = out_grad.shape[1] // HD
    score_scale = HD ** (-0.5)
    n_ctx = matching.shape[1]
    projected = jnp.dot(activations, w_qkv, preferred_element_type=f32).astype(jnp.bfloat16)
    projected = projected.reshape(local_tokens, head_count, 3, HD)
    query = to_blocks(projected[:, :, 0].reshape(local_tokens, head_count * HD), HD)
    key_own = to_blocks(projected[:, :, 1].reshape(local_tokens, head_count * HD), HD)
    value_own = to_blocks(projected[:, :, 2].reshape(local_tokens, head_count * HD), HD)
    order = matching[0]
    inverse = jnp.zeros_like(order).at[order].set(jnp.arange(n_ctx, dtype=order.dtype))
    own_kv = jnp.stack([key_own, value_own], 0)
    far_kv = from_pieces(route(to_pieces(own_kv, n_ctx), order))
    key_far, value_far = far_kv[0], far_kv[1]

    def mm(form, left, right):
        return jnp.einsum(form, left, right, preferred_element_type=f32)

    score_own = mm("hnqd,hnkd->hnqk", query, key_own) * score_scale
    score_far = mm("hnqd,hnkd->hnqk", query, key_far) * score_scale
    row_max = jnp.maximum(jnp.max(score_own, -1, keepdims=True), jnp.max(score_far, -1, keepdims=True))
    total = jnp.sum(jnp.exp(score_own - row_max), -1, keepdims=True) + jnp.sum(
        jnp.exp(score_far - row_max), -1, keepdims=True
    )
    log_total = row_max + jnp.log(total)
    prob_own = jnp.exp(score_own - log_total)
    prob_far = jnp.exp(score_far - log_total)
    words = to_blocks(dropout_bits, WORDS)
    half_words = WORDS // 2
    kept_own = unpack_bits(words[..., :half_words])
    kept_far = unpack_bits(words[..., half_words:])
    dropped_own = (prob_own * kept_own).astype(jnp.bfloat16)
    dropped_far = (prob_far * kept_far).astype(jnp.bfloat16)
    attended = (
        mm("hnqk,hnkd->hnqd", dropped_own, value_own) + mm("hnqk,hnkd->hnqd", dropped_far, value_far)
    ).astype(jnp.bfloat16)
    grad_out = to_blocks(out_grad, HD)
    grad_prob_own = mm("hnqd,hnkd->hnqk", grad_out, value_own) * kept_own
    grad_prob_far = mm("hnqd,hnkd->hnqk", grad_out, value_far) * kept_far
    row_delta = jnp.sum(prob_own * grad_prob_own, -1, keepdims=True) + jnp.sum(
        prob_far * grad_prob_far, -1, keepdims=True
    )
    score_grad_own = (prob_own * (grad_prob_own - row_delta) * score_scale).astype(jnp.bfloat16)
    score_grad_far = (prob_far * (grad_prob_far - row_delta) * score_scale).astype(jnp.bfloat16)
    grad_query = (
        mm("hnqk,hnkd->hnqd", score_grad_own, key_own) + mm("hnqk,hnkd->hnqd", score_grad_far, key_far)
    ).astype(jnp.bfloat16)
    grad_key_own = mm("hnqk,hnqd->hnkd", score_grad_own, query)
    grad_value_own = mm("hnqk,hnqd->hnkd", dropped_own, grad_out)
    far_part = jnp.stack(
        [mm("hnqk,hnqd->hnkd", score_grad_far, query), mm("hnqk,hnqd->hnkd", dropped_far, grad_out)], 0
    ).astype(jnp.bfloat16)
    returned = from_pieces(route(to_pieces(far_part, n_ctx), inverse))
    grad_key = (grad_key_own + returned[0].astype(f32)).astype(jnp.bfloat16)
    grad_value = (grad_value_own + returned[1].astype(f32)).astype(jnp.bfloat16)
    stacked = jnp.stack([grad_query, grad_key, grad_value], 3)
    grad_qkv = stacked.transpose(1, 2, 0, 3, 4).reshape(local_tokens, head_count * 3 * HD)
    query_cols = grad_query.transpose(1, 2, 0, 3).reshape(local_tokens, head_count * HD)
    kv_cols = jnp.stack([grad_key, grad_value], 3).transpose(1, 2, 0, 3, 4)
    kv_cols = kv_cols.reshape(local_tokens, head_count * 2 * HD)
    weight_q = reduce_ctx(weight_term(activations, query_cols))
    weight_kv = reduce_ctx(weight_term(activations, kv_cols))
    rows = weight_q.shape[0]
    weight_grad = jnp.concatenate(
        [weight_q.reshape(rows, head_count, 1, HD), weight_kv.reshape(rows, head_count, 2, HD)], 2
    ).reshape(rows, head_count * 3 * HD)
    n_y = lax.psum(1, "y")
    width = activations.shape[1] // (2 * n_y)
    w_split = w_qkv.reshape(n_y, 2, width, w_qkv.shape[1])
    by_core = jnp.einsum("tk,ycwk->cytw", grad_qkv, w_split, preferred_element_type=f32)
    core_sum = ring_rs(by_core.astype(jnp.bfloat16), "c", 2)
    input_grad = ring_rs(core_sum, "y", n_y)
    return (from_blocks(attended), input_grad, weight_grad)


def solution(mesh):
    n_ctx, n_tp = mesh.devices.shape
    n_x = 4 if n_ctx % 4 == 0 else 1
    fine = Mesh(mesh.devices.reshape(n_ctx // n_x, n_x, n_tp // 2, 2), ("z", "x", "y", "c"))
    return jax.shard_map(
        per_device,
        mesh=fine,
        in_specs=(P(CTX, None), P(None, TP), P(TP, None), P(CTX, TP), P(CTX, TP)),
        out_specs=(P(CTX, TP), P(CTX, TP), P(CTX, TP)),
        check_vma=False,
    )
```

```python
import jax
import jax.numpy as jnp
import numpy as np
from jax import lax
from jax.sharding import Mesh, PartitionSpec as P

HD = 128
BLK = 256
HGROUP = 2
WORDS = 32


def unpack_bits(words):
    shifts = jnp.arange(16, dtype=jnp.int32)
    bits = jnp.bitwise_and(jnp.right_shift(words[..., None], shifts), 1)
    return bits.reshape(words.shape[:-1] + (words.shape[-1] * 16,)).astype(jnp.float32) * 2.0


def to_blocks(flat, width):
    row_total = flat.shape[0]
    head_count = flat.shape[1] // width
    return flat.reshape(row_total // BLK, BLK, head_count, width).transpose(2, 0, 1, 3)


def from_blocks(blocked):
    head_count, block_count, block_rows, width = blocked.shape
    return blocked.transpose(1, 2, 0, 3).reshape(block_count * block_rows, head_count * width)


CTX = ("z", "x")
TP = ("y", "c")


def route(payload, order):
    spread = lax.all_to_all(payload, CTX, 0, 0, tiled=True)
    pieces = spread.shape[0]
    pick = (order[:, None] == jnp.arange(pieces, dtype=order.dtype)[None, :]).astype(spread.dtype)
    flat = spread.reshape(pieces, -1)
    chosen = jnp.dot(pick, flat, preferred_element_type=jnp.float32).astype(spread.dtype)
    return lax.all_to_all(chosen.reshape(spread.shape), CTX, 0, 0, tiled=True)


def to_pieces(blocked, pieces):
    lead = blocked.shape[:-2]
    rows, width = blocked.shape[-2:]
    split = blocked.reshape(lead + (pieces, rows // pieces, width))
    return jnp.moveaxis(split, len(lead), 0)


def from_pieces(spread):
    joined = jnp.moveaxis(spread, 0, -3)
    return joined.reshape(joined.shape[:-3] + (-1, joined.shape[-1]))


def ring_rs(chunks, axis, n):
    i = lax.axis_index(axis)
    if n == 2:
        other = lax.dynamic_index_in_dim(chunks, 1 - i, 0, keepdims=False)
        mine = lax.dynamic_index_in_dim(chunks, i, 0, keepdims=False)
        got = lax.ppermute(other, axis, [(0, 1), (1, 0)])
        return (got.astype(jnp.float32) + mine.astype(jnp.float32)).astype(chunks.dtype)
    half = chunks.shape[1] // 2
    cw = [(j, (j + 1) % n) for j in range(n)]
    ccw = [(j, (j - 1) % n) for j in range(n)]

    def take(k, part):
        block = lax.dynamic_index_in_dim(chunks, k % n, 0, keepdims=False)
        return block[:half] if part == 0 else block[half:]

    acc_a = take(i - 1 + n, 0)
    acc_b = take(i + 1, 1)
    for s in range(n - 1):
        got_a = lax.ppermute(acc_a, axis, cw)
        got_b = lax.ppermute(acc_b, axis, ccw)
        acc_a = (got_a.astype(jnp.float32) + take(i - s - 2 + 2 * n, 0).astype(jnp.float32)).astype(chunks.dtype)
        acc_b = (got_b.astype(jnp.float32) + take(i + s + 2, 1).astype(jnp.float32)).astype(chunks.dtype)
    return jnp.concatenate([acc_a, acc_b], 0)


def weight_term(activations, cols):
    return lax.dot_general(
        activations, cols, (((0,), (0,)), ((), ())), preferred_element_type=jnp.float32
    ).astype(jnp.bfloat16)


def reduce_ctx(part):
    part = lax.psum_scatter(part, "z", scatter_dimension=0, tiled=True)
    n_x = lax.psum(1, "x")
    pieces = part.reshape((n_x, part.shape[0] // n_x) + part.shape[1:])
    gathered = lax.all_to_all(pieces, "x", 0, 0, tiled=True)
    return jnp.sum(gathered.astype(jnp.float32), 0).astype(part.dtype)


def per_device(activations, w_qkv, matching, dropout_bits, out_grad):
    f32 = jnp.float32
    local_tokens = activations.shape[0]
    head_count = out_grad.shape[1] // HD
    score_scale = HD ** (-0.5)
    n_ctx = matching.shape[1]
    projected = jnp.dot(activations, w_qkv, preferred_element_type=f32).astype(jnp.bfloat16)
    projected = projected.reshape(local_tokens, head_count, 3, HD)
    query = to_blocks(projected[:, :, 0].reshape(local_tokens, head_count * HD), HD)
    key_own = to_blocks(projected[:, :, 1].reshape(local_tokens, head_count * HD), HD)
    value_own = to_blocks(projected[:, :, 2].reshape(local_tokens, head_count * HD), HD)
    order = matching[0]
    inverse = jnp.zeros_like(order).at[order].set(jnp.arange(n_ctx, dtype=order.dtype))
    far_rows = from_pieces(route(to_pieces(activations, n_ctx), order))
    own_kv = jnp.stack([key_own, value_own], 0)
    far_kv = from_pieces(route(to_pieces(own_kv, n_ctx), order))
    far_rows, far_kv = lax.optimization_barrier((far_rows, far_kv))
    key_far, value_far = far_kv[0], far_kv[1]

    def mm(form, left, right):
        return jnp.einsum(form, left, right, preferred_element_type=f32)

    score_own = mm("hnqd,hnkd->hnqk", query, key_own) * score_scale
    score_far = mm("hnqd,hnkd->hnqk", query, key_far) * score_scale
    row_max = jnp.maximum(jnp.max(score_own, -1, keepdims=True), jnp.max(score_far, -1, keepdims=True))
    total = jnp.sum(jnp.exp(score_own - row_max), -1, keepdims=True) + jnp.sum(
        jnp.exp(score_far - row_max), -1, keepdims=True
    )
    log_total = row_max + jnp.log(total)
    prob_own = jnp.exp(score_own - log_total)
    prob_far = jnp.exp(score_far - log_total)
    words = to_blocks(dropout_bits, WORDS)
    half_words = WORDS // 2
    kept_own = unpack_bits(words[..., :half_words])
    kept_far = unpack_bits(words[..., half_words:])
    dropped_own = (prob_own * kept_own).astype(jnp.bfloat16)
    dropped_far = (prob_far * kept_far).astype(jnp.bfloat16)
    attended = (
        mm("hnqk,hnkd->hnqd", dropped_own, value_own) + mm("hnqk,hnkd->hnqd", dropped_far, value_far)
    ).astype(jnp.bfloat16)
    grad_out = to_blocks(out_grad, HD)
    grad_prob_own = mm("hnqd,hnkd->hnqk", grad_out, value_own) * kept_own
    grad_prob_far = mm("hnqd,hnkd->hnqk", grad_out, value_far) * kept_far
    row_delta = jnp.sum(prob_own * grad_prob_own, -1, keepdims=True) + jnp.sum(
        prob_far * grad_prob_far, -1, keepdims=True
    )
    score_grad_own = (prob_own * (grad_prob_own - row_delta) * score_scale).astype(jnp.bfloat16)
    score_grad_far = (prob_far * (grad_prob_far - row_delta) * score_scale).astype(jnp.bfloat16)
    grad_query = (
        mm("hnqk,hnkd->hnqd", score_grad_own, key_own) + mm("hnqk,hnkd->hnqd", score_grad_far, key_far)
    ).astype(jnp.bfloat16)
    grad_key_own = mm("hnqk,hnqd->hnkd", score_grad_own, query)
    grad_value_own = mm("hnqk,hnqd->hnkd", dropped_own, grad_out)
    far_part = jnp.stack(
        [mm("hnqk,hnqd->hnkd", score_grad_far, query), mm("hnqk,hnqd->hnkd", dropped_far, grad_out)], 0
    ).astype(jnp.bfloat16)
    near_cols = jnp.stack(
        [grad_query.astype(f32), grad_key_own, grad_value_own], 3
    ).transpose(1, 2, 0, 3, 4).reshape(local_tokens, head_count * 3 * HD)
    far_cols = jnp.concatenate(
        [jnp.zeros((1,) + far_part.shape[1:], far_part.dtype), far_part], 0
    ).transpose(2, 3, 1, 0, 4).reshape(local_tokens, head_count * 3 * HD)
    both_rows = jnp.concatenate([activations, far_rows], 0)
    both_cols = jnp.concatenate([near_cols.astype(jnp.bfloat16), far_cols], 0)
    weight_part = weight_term(both_rows, both_cols)
    far_part, weight_part = lax.optimization_barrier((far_part, weight_part))
    returned = from_pieces(route(to_pieces(far_part, n_ctx), inverse))
    grad_key = (grad_key_own + returned[0].astype(f32)).astype(jnp.bfloat16)
    grad_value = (grad_value_own + returned[1].astype(f32)).astype(jnp.bfloat16)
    stacked = jnp.stack([grad_query, grad_key, grad_value], 3)
    grad_qkv = stacked.transpose(1, 2, 0, 3, 4).reshape(local_tokens, head_count * 3 * HD)
    weight_grad = reduce_ctx(weight_part)
    n_y = lax.psum(1, "y")
    width = activations.shape[1] // (2 * n_y)
    w_split = w_qkv.reshape(n_y, 2, width, w_qkv.shape[1])
    by_core = jnp.einsum("tk,ycwk->cytw", grad_qkv, w_split, preferred_element_type=f32)
    core_sum = ring_rs(by_core.astype(jnp.bfloat16), "c", 2)
    input_grad = ring_rs(core_sum, "y", n_y)
    return (from_blocks(attended), input_grad, weight_grad)


def solution(mesh):
    n_ctx, n_tp = mesh.devices.shape
    n_x = 4 if n_ctx % 4 == 0 else 1
    fine = Mesh(mesh.devices.reshape(n_ctx // n_x, n_x, n_tp // 2, 2), ("z", "x", "y", "c"))
    return jax.shard_map(
        per_device,
        mesh=fine,
        in_specs=(P(CTX, None), P(None, TP), P(TP, None), P(CTX, TP), P(CTX, TP)),
        out_specs=(P(CTX, TP), P(CTX, TP), P(CTX, TP)),
        check_vma=False,
    )
```

```python
import jax
import jax.numpy as jnp
import numpy as np
from jax import lax
from jax.sharding import Mesh, PartitionSpec as P

HD = 128
BLK = 256
HGROUP = 2
WORDS = 32


def unpack_bits(words):
    shifts = jnp.arange(16, dtype=jnp.int32)
    bits = jnp.bitwise_and(jnp.right_shift(words[..., None], shifts), 1)
    return bits.reshape(words.shape[:-1] + (words.shape[-1] * 16,)).astype(jnp.float32) * 2.0


def to_blocks(flat, width):
    row_total = flat.shape[0]
    head_count = flat.shape[1] // width
    return flat.reshape(row_total // BLK, BLK, head_count, width).transpose(2, 0, 1, 3)


def from_blocks(blocked):
    head_count, block_count, block_rows, width = blocked.shape
    return blocked.transpose(1, 2, 0, 3).reshape(block_count * block_rows, head_count * width)


CTX = ("z", "x")
TP = ("y", "c")


def route(payload, order):
    spread = lax.all_to_all(payload, CTX, 0, 0, tiled=True)
    pieces = spread.shape[0]
    pick = (order[:, None] == jnp.arange(pieces, dtype=order.dtype)[None, :]).astype(spread.dtype)
    flat = spread.reshape(pieces, -1)
    chosen = jnp.dot(pick, flat, preferred_element_type=jnp.float32).astype(spread.dtype)
    return lax.all_to_all(chosen.reshape(spread.shape), CTX, 0, 0, tiled=True)


def to_pieces(blocked, pieces):
    lead = blocked.shape[:-2]
    rows, width = blocked.shape[-2:]
    split = blocked.reshape(lead + (pieces, rows // pieces, width))
    return jnp.moveaxis(split, len(lead), 0)


def from_pieces(spread):
    joined = jnp.moveaxis(spread, 0, -3)
    return joined.reshape(joined.shape[:-3] + (-1, joined.shape[-1]))


def ring_rs(chunks, axis, n):
    i = lax.axis_index(axis)
    if n == 2:
        other = lax.dynamic_index_in_dim(chunks, 1 - i, 0, keepdims=False)
        mine = lax.dynamic_index_in_dim(chunks, i, 0, keepdims=False)
        got = lax.ppermute(other, axis, [(0, 1), (1, 0)])
        return (got.astype(jnp.float32) + mine.astype(jnp.float32)).astype(chunks.dtype)
    half = chunks.shape[1] // 2
    cw = [(j, (j + 1) % n) for j in range(n)]
    ccw = [(j, (j - 1) % n) for j in range(n)]

    def take(k, part):
        block = lax.dynamic_index_in_dim(chunks, k % n, 0, keepdims=False)
        return block[:half] if part == 0 else block[half:]

    acc_a = take(i - 1 + n, 0)
    acc_b = take(i + 1, 1)
    for s in range(n - 1):
        got_a = lax.ppermute(acc_a, axis, cw)
        got_b = lax.ppermute(acc_b, axis, ccw)
        acc_a = (got_a.astype(jnp.float32) + take(i - s - 2 + 2 * n, 0).astype(jnp.float32)).astype(chunks.dtype)
        acc_b = (got_b.astype(jnp.float32) + take(i + s + 2, 1).astype(jnp.float32)).astype(chunks.dtype)
    return jnp.concatenate([acc_a, acc_b], 0)


def weight_term(activations, cols):
    return lax.dot_general(
        activations, cols, (((0,), (0,)), ((), ())), preferred_element_type=jnp.float32
    ).astype(jnp.bfloat16)


def reduce_ctx(part):
    return reduce_x(lax.psum_scatter(part, "z", scatter_dimension=0, tiled=True))


def reduce_x(part):
    n_x = lax.psum(1, "x")
    pieces = part.reshape((n_x, part.shape[0] // n_x) + part.shape[1:])
    gathered = lax.all_to_all(pieces, "x", 0, 0, tiled=True)
    return jnp.sum(gathered.astype(jnp.float32), 0).astype(part.dtype)


def per_device(activations, w_qkv, matching, dropout_bits, out_grad):
    f32 = jnp.float32
    local_tokens = activations.shape[0]
    head_count = out_grad.shape[1] // HD
    score_scale = HD ** (-0.5)
    n_ctx = matching.shape[1]
    projected = jnp.dot(activations, w_qkv, preferred_element_type=f32).astype(jnp.bfloat16)
    projected = projected.reshape(local_tokens, head_count, 3, HD)
    query = to_blocks(projected[:, :, 0].reshape(local_tokens, head_count * HD), HD)
    key_own = to_blocks(projected[:, :, 1].reshape(local_tokens, head_count * HD), HD)
    value_own = to_blocks(projected[:, :, 2].reshape(local_tokens, head_count * HD), HD)
    order = matching[0]
    inverse = jnp.zeros_like(order).at[order].set(jnp.arange(n_ctx, dtype=order.dtype))
    own_kv = jnp.stack([key_own, value_own], 0)
    far_kv = from_pieces(route(to_pieces(own_kv, n_ctx), order))
    key_far, value_far = far_kv[0], far_kv[1]

    def mm(form, left, right):
        return jnp.einsum(form, left, right, preferred_element_type=f32)

    score_own = mm("hnqd,hnkd->hnqk", query, key_own) * score_scale
    score_far = mm("hnqd,hnkd->hnqk", query, key_far) * score_scale
    row_max = jnp.maximum(jnp.max(score_own, -1, keepdims=True), jnp.max(score_far, -1, keepdims=True))
    total = jnp.sum(jnp.exp(score_own - row_max), -1, keepdims=True) + jnp.sum(
        jnp.exp(score_far - row_max), -1, keepdims=True
    )
    log_total = row_max + jnp.log(total)
    prob_own = jnp.exp(score_own - log_total)
    prob_far = jnp.exp(score_far - log_total)
    words = to_blocks(dropout_bits, WORDS)
    half_words = WORDS // 2
    kept_own = unpack_bits(words[..., :half_words])
    kept_far = unpack_bits(words[..., half_words:])
    dropped_own = (prob_own * kept_own).astype(jnp.bfloat16)
    dropped_far = (prob_far * kept_far).astype(jnp.bfloat16)
    attended = (
        mm("hnqk,hnkd->hnqd", dropped_own, value_own) + mm("hnqk,hnkd->hnqd", dropped_far, value_far)
    ).astype(jnp.bfloat16)
    grad_out = to_blocks(out_grad, HD)
    grad_prob_own = mm("hnqd,hnkd->hnqk", grad_out, value_own) * kept_own
    grad_prob_far = mm("hnqd,hnkd->hnqk", grad_out, value_far) * kept_far
    row_delta = jnp.sum(prob_own * grad_prob_own, -1, keepdims=True) + jnp.sum(
        prob_far * grad_prob_far, -1, keepdims=True
    )
    score_grad_own = (prob_own * (grad_prob_own - row_delta) * score_scale).astype(jnp.bfloat16)
    score_grad_far = (prob_far * (grad_prob_far - row_delta) * score_scale).astype(jnp.bfloat16)
    grad_query = (
        mm("hnqk,hnkd->hnqd", score_grad_own, key_own) + mm("hnqk,hnkd->hnqd", score_grad_far, key_far)
    ).astype(jnp.bfloat16)
    grad_key_own = mm("hnqk,hnqd->hnkd", score_grad_own, query)
    grad_value_own = mm("hnqk,hnqd->hnkd", dropped_own, grad_out)
    far_part = jnp.stack(
        [mm("hnqk,hnqd->hnkd", score_grad_far, query), mm("hnqk,hnqd->hnkd", dropped_far, grad_out)], 0
    ).astype(jnp.bfloat16)
    returned = from_pieces(route(to_pieces(far_part, n_ctx), inverse))
    grad_key = (grad_key_own + returned[0].astype(f32)).astype(jnp.bfloat16)
    grad_value = (grad_value_own + returned[1].astype(f32)).astype(jnp.bfloat16)
    stacked = jnp.stack([grad_query, grad_key, grad_value], 3)
    grad_qkv = stacked.transpose(1, 2, 0, 3, 4).reshape(local_tokens, head_count * 3 * HD)
    query_cols = grad_query.transpose(1, 2, 0, 3).reshape(local_tokens, head_count * HD)
    kv_cols = jnp.stack([grad_key, grad_value], 3).transpose(1, 2, 0, 3, 4)
    kv_cols = kv_cols.reshape(local_tokens, head_count * 2 * HD)
    weight_q = reduce_ctx(weight_term(activations, query_cols))
    weight_kv = lax.psum_scatter(weight_term(activations, kv_cols), "z", scatter_dimension=0, tiled=True)
    n_y = lax.psum(1, "y")
    width = activations.shape[1] // (2 * n_y)
    w_split = w_qkv.reshape(n_y, 2, width, w_qkv.shape[1])
    by_core = jnp.einsum("tk,ycwk->cytw", grad_qkv, w_split, preferred_element_type=f32)
    core_sum = ring_rs(by_core.astype(jnp.bfloat16), "c", 2)
    input_grad = ring_rs(core_sum, "y", n_y)
    input_grad, weight_q, weight_kv = lax.optimization_barrier((input_grad, weight_q, weight_kv))
    weight_kv = reduce_x(weight_kv)
    rows = weight_q.shape[0]
    weight_grad = jnp.concatenate(
        [weight_q.reshape(rows, head_count, 1, HD), weight_kv.reshape(rows, head_count, 2, HD)], 2
    ).reshape(rows, head_count * 3 * HD)
    return (from_blocks(attended), input_grad, weight_grad)


def solution(mesh):
    n_ctx, n_tp = mesh.devices.shape
    n_x = 4 if n_ctx % 4 == 0 else 1
    fine = Mesh(mesh.devices.reshape(n_ctx // n_x, n_x, n_tp // 2, 2), ("z", "x", "y", "c"))
    return jax.shard_map(
        per_device,
        mesh=fine,
        in_specs=(P(CTX, None), P(None, TP), P(TP, None), P(CTX, TP), P(CTX, TP)),
        out_specs=(P(CTX, TP), P(CTX, TP), P(CTX, TP)),
        check_vma=False,
    )
```

```python
import jax
import jax.numpy as jnp
import numpy as np
from jax import lax
from jax.sharding import Mesh, PartitionSpec as P

HD = 128
BLK = 256
HGROUP = 2
WORDS = 32


def unpack_bits(words):
    shifts = jnp.arange(16, dtype=jnp.int32)
    bits = jnp.bitwise_and(jnp.right_shift(words[..., None], shifts), 1)
    return bits.reshape(words.shape[:-1] + (words.shape[-1] * 16,)).astype(jnp.float32) * 2.0


def to_blocks(flat, width):
    row_total = flat.shape[0]
    head_count = flat.shape[1] // width
    return flat.reshape(row_total // BLK, BLK, head_count, width).transpose(2, 0, 1, 3)


def from_blocks(blocked):
    head_count, block_count, block_rows, width = blocked.shape
    return blocked.transpose(1, 2, 0, 3).reshape(block_count * block_rows, head_count * width)


CTX = ("z", "x")
TP = ("y", "c")


def route(payload, order):
    spread = lax.all_to_all(payload, CTX, 0, 0, tiled=True)
    pieces = spread.shape[0]
    pick = (order[:, None] == jnp.arange(pieces, dtype=order.dtype)[None, :]).astype(spread.dtype)
    flat = spread.reshape(pieces, -1)
    chosen = jnp.dot(pick, flat, preferred_element_type=jnp.float32).astype(spread.dtype)
    return lax.all_to_all(chosen.reshape(spread.shape), CTX, 0, 0, tiled=True)


def to_pieces(blocked, pieces):
    lead = blocked.shape[:-2]
    rows, width = blocked.shape[-2:]
    split = blocked.reshape(lead + (pieces, rows // pieces, width))
    return jnp.moveaxis(split, len(lead), 0)


def from_pieces(spread):
    joined = jnp.moveaxis(spread, 0, -3)
    return joined.reshape(joined.shape[:-3] + (-1, joined.shape[-1]))


def ring_rs(chunks, axis, n):
    i = lax.axis_index(axis)
    if n == 2:
        other = lax.dynamic_index_in_dim(chunks, 1 - i, 0, keepdims=False)
        mine = lax.dynamic_index_in_dim(chunks, i, 0, keepdims=False)
        got = lax.ppermute(other, axis, [(0, 1), (1, 0)])
        return (got.astype(jnp.float32) + mine.astype(jnp.float32)).astype(chunks.dtype)
    half = chunks.shape[1] // 2
    cw = [(j, (j + 1) % n) for j in range(n)]
    ccw = [(j, (j - 1) % n) for j in range(n)]

    def take(k, part):
        block = lax.dynamic_index_in_dim(chunks, k % n, 0, keepdims=False)
        return block[:half] if part == 0 else block[half:]

    acc_a = take(i - 1 + n, 0)
    acc_b = take(i + 1, 1)
    for s in range(n - 1):
        got_a = lax.ppermute(acc_a, axis, cw)
        got_b = lax.ppermute(acc_b, axis, ccw)
        acc_a = (got_a.astype(jnp.float32) + take(i - s - 2 + 2 * n, 0).astype(jnp.float32)).astype(chunks.dtype)
        acc_b = (got_b.astype(jnp.float32) + take(i + s + 2, 1).astype(jnp.float32)).astype(chunks.dtype)
    return jnp.concatenate([acc_a, acc_b], 0)


def weight_term(activations, cols):
    return lax.dot_general(
        activations, cols, (((0,), (0,)), ((), ())), preferred_element_type=jnp.float32
    ).astype(jnp.bfloat16)


def reduce_ctx(part):
    return reduce_x(lax.psum_scatter(part, "z", scatter_dimension=0, tiled=True))


def reduce_x(part):
    n_x = lax.psum(1, "x")
    pieces = part.reshape((n_x, part.shape[0] // n_x) + part.shape[1:])
    gathered = lax.all_to_all(pieces, "x", 0, 0, tiled=True)
    return jnp.sum(gathered.astype(jnp.float32), 0).astype(part.dtype)


def reduce_x_then_z(part):
    n_x = lax.psum(1, "x")
    n_z = lax.psum(1, "z")
    rows = part.shape[0] // (n_x * n_z)
    pieces = part.reshape(n_z, n_x, rows, part.shape[1]).transpose(1, 0, 2, 3)
    got = lax.all_to_all(pieces, "x", 0, 0, tiled=True)
    summed = jnp.sum(got.astype(jnp.float32), 0).astype(part.dtype)
    got = lax.all_to_all(summed, "z", 0, 0, tiled=True)
    return jnp.sum(got.astype(jnp.float32), 0).astype(part.dtype)


def per_device(activations, w_qkv, matching, dropout_bits, out_grad):
    f32 = jnp.float32
    local_tokens = activations.shape[0]
    head_count = out_grad.shape[1] // HD
    score_scale = HD ** (-0.5)
    n_ctx = matching.shape[1]
    projected = jnp.dot(activations, w_qkv, preferred_element_type=f32).astype(jnp.bfloat16)
    projected = projected.reshape(local_tokens, head_count, 3, HD)
    query = to_blocks(projected[:, :, 0].reshape(local_tokens, head_count * HD), HD)
    key_own = to_blocks(projected[:, :, 1].reshape(local_tokens, head_count * HD), HD)
    value_own = to_blocks(projected[:, :, 2].reshape(local_tokens, head_count * HD), HD)
    order = matching[0]
    inverse = jnp.zeros_like(order).at[order].set(jnp.arange(n_ctx, dtype=order.dtype))
    own_kv = jnp.stack([key_own, value_own], 0)
    far_kv = from_pieces(route(to_pieces(own_kv, n_ctx), order))
    key_far, value_far = far_kv[0], far_kv[1]

    def mm(form, left, right):
        return jnp.einsum(form, left, right, preferred_element_type=f32)

    score_own = mm("hnqd,hnkd->hnqk", query, key_own) * score_scale
    score_far = mm("hnqd,hnkd->hnqk", query, key_far) * score_scale
    row_max = jnp.maximum(jnp.max(score_own, -1, keepdims=True), jnp.max(score_far, -1, keepdims=True))
    total = jnp.sum(jnp.exp(score_own - row_max), -1, keepdims=True) + jnp.sum(
        jnp.exp(score_far - row_max), -1, keepdims=True
    )
    log_total = row_max + jnp.log(total)
    prob_own = jnp.exp(score_own - log_total)
    prob_far = jnp.exp(score_far - log_total)
    words = to_blocks(dropout_bits, WORDS)
    half_words = WORDS // 2
    kept_own = unpack_bits(words[..., :half_words])
    kept_far = unpack_bits(words[..., half_words:])
    dropped_own = (prob_own * kept_own).astype(jnp.bfloat16)
    dropped_far = (prob_far * kept_far).astype(jnp.bfloat16)
    attended = (
        mm("hnqk,hnkd->hnqd", dropped_own, value_own) + mm("hnqk,hnkd->hnqd", dropped_far, value_far)
    ).astype(jnp.bfloat16)
    grad_out = to_blocks(out_grad, HD)
    grad_prob_own = mm("hnqd,hnkd->hnqk", grad_out, value_own) * kept_own
    grad_prob_far = mm("hnqd,hnkd->hnqk", grad_out, value_far) * kept_far
    row_delta = jnp.sum(prob_own * grad_prob_own, -1, keepdims=True) + jnp.sum(
        prob_far * grad_prob_far, -1, keepdims=True
    )
    score_grad_own = (prob_own * (grad_prob_own - row_delta) * score_scale).astype(jnp.bfloat16)
    score_grad_far = (prob_far * (grad_prob_far - row_delta) * score_scale).astype(jnp.bfloat16)
    grad_query = (
        mm("hnqk,hnkd->hnqd", score_grad_own, key_own) + mm("hnqk,hnkd->hnqd", score_grad_far, key_far)
    ).astype(jnp.bfloat16)
    grad_key_own = mm("hnqk,hnqd->hnkd", score_grad_own, query)
    grad_value_own = mm("hnqk,hnqd->hnkd", dropped_own, grad_out)
    far_part = jnp.stack(
        [mm("hnqk,hnqd->hnkd", score_grad_far, query), mm("hnqk,hnqd->hnkd", dropped_far, grad_out)], 0
    ).astype(jnp.bfloat16)
    returned = from_pieces(route(to_pieces(far_part, n_ctx), inverse))
    grad_key = (grad_key_own + returned[0].astype(f32)).astype(jnp.bfloat16)
    grad_value = (grad_value_own + returned[1].astype(f32)).astype(jnp.bfloat16)
    stacked = jnp.stack([grad_query, grad_key, grad_value], 3)
    grad_qkv = stacked.transpose(1, 2, 0, 3, 4).reshape(local_tokens, head_count * 3 * HD)
    query_cols = grad_query.transpose(1, 2, 0, 3).reshape(local_tokens, head_count * HD)
    kv_cols = jnp.stack([grad_key, grad_value], 3).transpose(1, 2, 0, 3, 4)
    kv_cols = kv_cols.reshape(local_tokens, head_count * 2 * HD)
    weight_q = reduce_ctx(weight_term(activations, query_cols))
    kv_part = weight_term(activations, kv_cols)
    side = kv_part.shape[1] // 4
    weight_side = reduce_x_then_z(kv_part[:, -side:])
    weight_kv = lax.psum_scatter(kv_part[:, :-side], "z", scatter_dimension=0, tiled=True)
    n_y = lax.psum(1, "y")
    width = activations.shape[1] // (2 * n_y)
    w_split = w_qkv.reshape(n_y, 2, width, w_qkv.shape[1])
    by_core = jnp.einsum("tk,ycwk->cytw", grad_qkv, w_split, preferred_element_type=f32)
    core_sum = ring_rs(by_core.astype(jnp.bfloat16), "c", 2)
    input_grad = ring_rs(core_sum, "y", n_y)
    weight_side, weight_q, weight_kv = lax.optimization_barrier((weight_side, weight_q, weight_kv))
    weight_kv = jnp.concatenate([reduce_x(weight_kv), weight_side], 1)
    rows = weight_q.shape[0]
    weight_grad = jnp.concatenate(
        [weight_q.reshape(rows, head_count, 1, HD), weight_kv.reshape(rows, head_count, 2, HD)], 2
    ).reshape(rows, head_count * 3 * HD)
    return (from_blocks(attended), input_grad, weight_grad)


def solution(mesh):
    n_ctx, n_tp = mesh.devices.shape
    n_x = 4 if n_ctx % 4 == 0 else 1
    fine = Mesh(mesh.devices.reshape(n_ctx // n_x, n_x, n_tp // 2, 2), ("z", "x", "y", "c"))
    return jax.shard_map(
        per_device,
        mesh=fine,
        in_specs=(P(CTX, None), P(None, TP), P(TP, None), P(CTX, TP), P(CTX, TP)),
        out_specs=(P(CTX, TP), P(CTX, TP), P(CTX, TP)),
        check_vma=False,
    )
```

```python
import jax
import jax.numpy as jnp
import numpy as np
from jax import lax
from jax.sharding import Mesh, PartitionSpec as P

HD = 128
BLK = 256
HGROUP = 2
WORDS = 32


def unpack_bits(words):
    shifts = jnp.arange(16, dtype=jnp.int32)
    bits = jnp.bitwise_and(jnp.right_shift(words[..., None], shifts), 1)
    return bits.reshape(words.shape[:-1] + (words.shape[-1] * 16,)).astype(jnp.float32) * 2.0


def to_blocks(flat, width):
    row_total = flat.shape[0]
    head_count = flat.shape[1] // width
    return flat.reshape(row_total // BLK, BLK, head_count, width).transpose(2, 0, 1, 3)


def from_blocks(blocked):
    head_count, block_count, block_rows, width = blocked.shape
    return blocked.transpose(1, 2, 0, 3).reshape(block_count * block_rows, head_count * width)


CTX = ("z", "x")
TP = ("y", "c")


def route(payload, order):
    spread = lax.all_to_all(payload, CTX, 0, 0, tiled=True)
    pieces = spread.shape[0]
    pick = (order[:, None] == jnp.arange(pieces, dtype=order.dtype)[None, :]).astype(spread.dtype)
    flat = spread.reshape(pieces, -1)
    chosen = jnp.dot(pick, flat, preferred_element_type=jnp.float32).astype(spread.dtype)
    return lax.all_to_all(chosen.reshape(spread.shape), CTX, 0, 0, tiled=True)


def to_pieces(blocked, pieces):
    lead = blocked.shape[:-2]
    rows, width = blocked.shape[-2:]
    split = blocked.reshape(lead + (pieces, rows // pieces, width))
    return jnp.moveaxis(split, len(lead), 0)


def from_pieces(spread):
    joined = jnp.moveaxis(spread, 0, -3)
    return joined.reshape(joined.shape[:-3] + (-1, joined.shape[-1]))


def ring_rs(chunks, axis, n):
    i = lax.axis_index(axis)
    if n == 2:
        other = lax.dynamic_index_in_dim(chunks, 1 - i, 0, keepdims=False)
        mine = lax.dynamic_index_in_dim(chunks, i, 0, keepdims=False)
        got = lax.ppermute(other, axis, [(0, 1), (1, 0)])
        return (got.astype(jnp.float32) + mine.astype(jnp.float32)).astype(chunks.dtype)
    half = chunks.shape[1] // 2
    cw = [(j, (j + 1) % n) for j in range(n)]
    ccw = [(j, (j - 1) % n) for j in range(n)]

    def take(k, part):
        block = lax.dynamic_index_in_dim(chunks, k % n, 0, keepdims=False)
        return block[:half] if part == 0 else block[half:]

    acc_a = take(i - 1 + n, 0)
    acc_b = take(i + 1, 1)
    for s in range(n - 1):
        got_a = lax.ppermute(acc_a, axis, cw)
        got_b = lax.ppermute(acc_b, axis, ccw)
        acc_a = (got_a.astype(jnp.float32) + take(i - s - 2 + 2 * n, 0).astype(jnp.float32)).astype(chunks.dtype)
        acc_b = (got_b.astype(jnp.float32) + take(i + s + 2, 1).astype(jnp.float32)).astype(chunks.dtype)
    return jnp.concatenate([acc_a, acc_b], 0)


def weight_term(activations, cols):
    return lax.dot_general(
        activations, cols, (((0,), (0,)), ((), ())), preferred_element_type=jnp.float32
    ).astype(jnp.bfloat16)


def reduce_ctx(part):
    return reduce_x(lax.psum_scatter(part, "z", scatter_dimension=0, tiled=True))


def reduce_x(part):
    n_x = lax.psum(1, "x")
    i = lax.axis_index("x")
    pieces = part.reshape((n_x, part.shape[0] // n_x) + part.shape[1:])
    total = lax.dynamic_index_in_dim(pieces, i, 0, keepdims=False).astype(jnp.float32)
    for s in range(1, n_x):
        outgoing = lax.dynamic_index_in_dim(pieces, (i + s) % n_x, 0, keepdims=False)
        total = total + lax.ppermute(outgoing, "x", [(j, (j + s) % n_x) for j in range(n_x)]).astype(jnp.float32)
    return total.astype(part.dtype)


def per_device(activations, w_qkv, matching, dropout_bits, out_grad):
    f32 = jnp.float32
    local_tokens = activations.shape[0]
    head_count = out_grad.shape[1] // HD
    score_scale = HD ** (-0.5)
    n_ctx = matching.shape[1]
    projected = jnp.dot(activations, w_qkv, preferred_element_type=f32).astype(jnp.bfloat16)
    projected = projected.reshape(local_tokens, head_count, 3, HD)
    query = to_blocks(projected[:, :, 0].reshape(local_tokens, head_count * HD), HD)
    key_own = to_blocks(projected[:, :, 1].reshape(local_tokens, head_count * HD), HD)
    value_own = to_blocks(projected[:, :, 2].reshape(local_tokens, head_count * HD), HD)
    order = matching[0]
    inverse = jnp.zeros_like(order).at[order].set(jnp.arange(n_ctx, dtype=order.dtype))
    own_kv = jnp.stack([key_own, value_own], 0)
    far_kv = from_pieces(route(to_pieces(own_kv, n_ctx), order))
    key_far, value_far = far_kv[0], far_kv[1]

    def mm(form, left, right):
        return jnp.einsum(form, left, right, preferred_element_type=f32)

    score_own = mm("hnqd,hnkd->hnqk", query, key_own) * score_scale
    score_far = mm("hnqd,hnkd->hnqk", query, key_far) * score_scale
    row_max = jnp.maximum(jnp.max(score_own, -1, keepdims=True), jnp.max(score_far, -1, keepdims=True))
    total = jnp.sum(jnp.exp(score_own - row_max), -1, keepdims=True) + jnp.sum(
        jnp.exp(score_far - row_max), -1, keepdims=True
    )
    log_total = row_max + jnp.log(total)
    prob_own = jnp.exp(score_own - log_total)
    prob_far = jnp.exp(score_far - log_total)
    words = to_blocks(dropout_bits, WORDS)
    half_words = WORDS // 2
    kept_own = unpack_bits(words[..., :half_words])
    kept_far = unpack_bits(words[..., half_words:])
    dropped_own = (prob_own * kept_own).astype(jnp.bfloat16)
    dropped_far = (prob_far * kept_far).astype(jnp.bfloat16)
    attended = (
        mm("hnqk,hnkd->hnqd", dropped_own, value_own) + mm("hnqk,hnkd->hnqd", dropped_far, value_far)
    ).astype(jnp.bfloat16)
    grad_out = to_blocks(out_grad, HD)
    grad_prob_own = mm("hnqd,hnkd->hnqk", grad_out, value_own) * kept_own
    grad_prob_far = mm("hnqd,hnkd->hnqk", grad_out, value_far) * kept_far
    row_delta = jnp.sum(prob_own * grad_prob_own, -1, keepdims=True) + jnp.sum(
        prob_far * grad_prob_far, -1, keepdims=True
    )
    score_grad_own = (prob_own * (grad_prob_own - row_delta) * score_scale).astype(jnp.bfloat16)
    score_grad_far = (prob_far * (grad_prob_far - row_delta) * score_scale).astype(jnp.bfloat16)
    grad_query = (
        mm("hnqk,hnkd->hnqd", score_grad_own, key_own) + mm("hnqk,hnkd->hnqd", score_grad_far, key_far)
    ).astype(jnp.bfloat16)
    grad_key_own = mm("hnqk,hnqd->hnkd", score_grad_own, query)
    grad_value_own = mm("hnqk,hnqd->hnkd", dropped_own, grad_out)
    far_part = jnp.stack(
        [mm("hnqk,hnqd->hnkd", score_grad_far, query), mm("hnqk,hnqd->hnkd", dropped_far, grad_out)], 0
    ).astype(jnp.bfloat16)
    returned = from_pieces(route(to_pieces(far_part, n_ctx), inverse))
    grad_key = (grad_key_own + returned[0].astype(f32)).astype(jnp.bfloat16)
    grad_value = (grad_value_own + returned[1].astype(f32)).astype(jnp.bfloat16)
    stacked = jnp.stack([grad_query, grad_key, grad_value], 3)
    grad_qkv = stacked.transpose(1, 2, 0, 3, 4).reshape(local_tokens, head_count * 3 * HD)
    query_cols = grad_query.transpose(1, 2, 0, 3).reshape(local_tokens, head_count * HD)
    kv_cols = jnp.stack([grad_key, grad_value], 3).transpose(1, 2, 0, 3, 4)
    kv_cols = kv_cols.reshape(local_tokens, head_count * 2 * HD)
    weight_q = reduce_ctx(weight_term(activations, query_cols))
    weight_kv = lax.psum_scatter(weight_term(activations, kv_cols), "z", scatter_dimension=0, tiled=True)
    n_y = lax.psum(1, "y")
    width = activations.shape[1] // (2 * n_y)
    w_split = w_qkv.reshape(n_y, 2, width, w_qkv.shape[1])
    by_core = jnp.einsum("tk,ycwk->cytw", grad_qkv, w_split, preferred_element_type=f32)
    core_sum = ring_rs(by_core.astype(jnp.bfloat16), "c", 2)
    input_grad = ring_rs(core_sum, "y", n_y)
    input_grad, weight_q, weight_kv = lax.optimization_barrier((input_grad, weight_q, weight_kv))
    weight_kv = reduce_x(weight_kv)
    rows = weight_q.shape[0]
    weight_grad = jnp.concatenate(
        [weight_q.reshape(rows, head_count, 1, HD), weight_kv.reshape(rows, head_count, 2, HD)], 2
    ).reshape(rows, head_count * 3 * HD)
    return (from_blocks(attended), input_grad, weight_grad)


def solution(mesh):
    n_ctx, n_tp = mesh.devices.shape
    n_x = 4 if n_ctx % 4 == 0 else 1
    fine = Mesh(mesh.devices.reshape(n_ctx // n_x, n_x, n_tp // 2, 2), ("z", "x", "y", "c"))
    return jax.shard_map(
        per_device,
        mesh=fine,
        in_specs=(P(CTX, None), P(None, TP), P(TP, None), P(CTX, TP), P(CTX, TP)),
        out_specs=(P(CTX, TP), P(CTX, TP), P(CTX, TP)),
        check_vma=False,
    )
```

```python
import jax
import jax.numpy as jnp
import numpy as np
from jax import lax
from jax.sharding import Mesh, PartitionSpec as P

HD = 128
BLK = 256
HGROUP = 2
WORDS = 32


def unpack_bits(words):
    shifts = jnp.arange(16, dtype=jnp.int32)
    bits = jnp.bitwise_and(jnp.right_shift(words[..., None], shifts), 1)
    return bits.reshape(words.shape[:-1] + (words.shape[-1] * 16,)).astype(jnp.float32) * 2.0


def to_blocks(flat, width):
    row_total = flat.shape[0]
    head_count = flat.shape[1] // width
    return flat.reshape(row_total // BLK, BLK, head_count, width).transpose(2, 0, 1, 3)


def from_blocks(blocked):
    head_count, block_count, block_rows, width = blocked.shape
    return blocked.transpose(1, 2, 0, 3).reshape(block_count * block_rows, head_count * width)


CTX = ("z", "x")
TP = ("y", "c")


def route(payload, order):
    spread = lax.all_to_all(payload, CTX, 0, 0, tiled=True)
    pieces = spread.shape[0]
    pick = (order[:, None] == jnp.arange(pieces, dtype=order.dtype)[None, :]).astype(spread.dtype)
    flat = spread.reshape(pieces, -1)
    chosen = jnp.dot(pick, flat, preferred_element_type=jnp.float32).astype(spread.dtype)
    return lax.all_to_all(chosen.reshape(spread.shape), CTX, 0, 0, tiled=True)


def to_pieces(blocked, pieces):
    lead = blocked.shape[:-2]
    rows, width = blocked.shape[-2:]
    split = blocked.reshape(lead + (pieces, rows // pieces, width))
    return jnp.moveaxis(split, len(lead), 0)


def from_pieces(spread):
    joined = jnp.moveaxis(spread, 0, -3)
    return joined.reshape(joined.shape[:-3] + (-1, joined.shape[-1]))


def ring_rs(chunks, axis, n):
    i = lax.axis_index(axis)
    if n == 2:
        other = lax.dynamic_index_in_dim(chunks, 1 - i, 0, keepdims=False)
        mine = lax.dynamic_index_in_dim(chunks, i, 0, keepdims=False)
        got = lax.ppermute(other, axis, [(0, 1), (1, 0)])
        return (got.astype(jnp.float32) + mine.astype(jnp.float32)).astype(chunks.dtype)
    half = chunks.shape[1] // 2
    cw = [(j, (j + 1) % n) for j in range(n)]
    ccw = [(j, (j - 1) % n) for j in range(n)]

    def take(k, part):
        block = lax.dynamic_index_in_dim(chunks, k % n, 0, keepdims=False)
        return block[:half] if part == 0 else block[half:]

    acc_a = take(i - 1 + n, 0)
    acc_b = take(i + 1, 1)
    for s in range(n - 1):
        got_a = lax.ppermute(acc_a, axis, cw)
        got_b = lax.ppermute(acc_b, axis, ccw)
        acc_a = (got_a.astype(jnp.float32) + take(i - s - 2 + 2 * n, 0).astype(jnp.float32)).astype(chunks.dtype)
        acc_b = (got_b.astype(jnp.float32) + take(i + s + 2, 1).astype(jnp.float32)).astype(chunks.dtype)
    return jnp.concatenate([acc_a, acc_b], 0)


def weight_term(activations, cols):
    return lax.dot_general(
        activations, cols, (((0,), (0,)), ((), ())), preferred_element_type=jnp.float32
    ).astype(jnp.bfloat16)


def reduce_ctx(part):
    return reduce_x(lax.psum_scatter(part, "z", scatter_dimension=0, tiled=True))


def reduce_x(part):
    n_x = lax.psum(1, "x")
    pieces = part.reshape((n_x, part.shape[0] // n_x) + part.shape[1:])
    gathered = lax.all_to_all(pieces, "x", 0, 0, tiled=True)
    return jnp.sum(gathered.astype(jnp.float32), 0).astype(part.dtype)


def per_device(activations, w_qkv, matching, dropout_bits, out_grad):
    f32 = jnp.float32
    local_tokens = activations.shape[0]
    head_count = out_grad.shape[1] // HD
    score_scale = HD ** (-0.5)
    n_ctx = matching.shape[1]
    w_heads = w_qkv.reshape(w_qkv.shape[0], head_count, 3, HD)
    kv_proj = jnp.einsum("tk,khcd->thcd", activations, w_heads[:, :, 1:], preferred_element_type=f32)
    kv_proj = kv_proj.astype(jnp.bfloat16)
    key_own = to_blocks(kv_proj[:, :, 0].reshape(local_tokens, head_count * HD), HD)
    value_own = to_blocks(kv_proj[:, :, 1].reshape(local_tokens, head_count * HD), HD)
    q_proj = jnp.einsum("tk,khd->thd", activations, w_heads[:, :, 0], preferred_element_type=f32)
    query = to_blocks(q_proj.astype(jnp.bfloat16).reshape(local_tokens, head_count * HD), HD)
    order = matching[0]
    inverse = jnp.zeros_like(order).at[order].set(jnp.arange(n_ctx, dtype=order.dtype))
    own_kv = jnp.stack([key_own, value_own], 0)
    far_kv = from_pieces(route(to_pieces(own_kv, n_ctx), order))
    key_far, value_far = far_kv[0], far_kv[1]

    def mm(form, left, right):
        return jnp.einsum(form, left, right, preferred_element_type=f32)

    score_own = mm("hnqd,hnkd->hnqk", query, key_own) * score_scale
    score_far = mm("hnqd,hnkd->hnqk", query, key_far) * score_scale
    row_max = jnp.maximum(jnp.max(score_own, -1, keepdims=True), jnp.max(score_far, -1, keepdims=True))
    total = jnp.sum(jnp.exp(score_own - row_max), -1, keepdims=True) + jnp.sum(
        jnp.exp(score_far - row_max), -1, keepdims=True
    )
    log_total = row_max + jnp.log(total)
    prob_own = jnp.exp(score_own - log_total)
    prob_far = jnp.exp(score_far - log_total)
    words = to_blocks(dropout_bits, WORDS)
    half_words = WORDS // 2
    kept_own = unpack_bits(words[..., :half_words])
    kept_far = unpack_bits(words[..., half_words:])
    dropped_own = (prob_own * kept_own).astype(jnp.bfloat16)
    dropped_far = (prob_far * kept_far).astype(jnp.bfloat16)
    attended = (
        mm("hnqk,hnkd->hnqd", dropped_own, value_own) + mm("hnqk,hnkd->hnqd", dropped_far, value_far)
    ).astype(jnp.bfloat16)
    grad_out = to_blocks(out_grad, HD)
    grad_prob_own = mm("hnqd,hnkd->hnqk", grad_out, value_own) * kept_own
    grad_prob_far = mm("hnqd,hnkd->hnqk", grad_out, value_far) * kept_far
    row_delta = jnp.sum(prob_own * grad_prob_own, -1, keepdims=True) + jnp.sum(
        prob_far * grad_prob_far, -1, keepdims=True
    )
    score_grad_own = (prob_own * (grad_prob_own - row_delta) * score_scale).astype(jnp.bfloat16)
    score_grad_far = (prob_far * (grad_prob_far - row_delta) * score_scale).astype(jnp.bfloat16)
    grad_query = (
        mm("hnqk,hnkd->hnqd", score_grad_own, key_own) + mm("hnqk,hnkd->hnqd", score_grad_far, key_far)
    ).astype(jnp.bfloat16)
    grad_key_own = mm("hnqk,hnqd->hnkd", score_grad_own, query)
    grad_value_own = mm("hnqk,hnqd->hnkd", dropped_own, grad_out)
    far_part = jnp.stack(
        [mm("hnqk,hnqd->hnkd", score_grad_far, query), mm("hnqk,hnqd->hnkd", dropped_far, grad_out)], 0
    ).astype(jnp.bfloat16)
    returned = from_pieces(route(to_pieces(far_part, n_ctx), inverse))
    grad_key = (grad_key_own + returned[0].astype(f32)).astype(jnp.bfloat16)
    grad_value = (grad_value_own + returned[1].astype(f32)).astype(jnp.bfloat16)
    stacked = jnp.stack([grad_query, grad_key, grad_value], 3)
    grad_qkv = stacked.transpose(1, 2, 0, 3, 4).reshape(local_tokens, head_count * 3 * HD)
    query_cols = grad_query.transpose(1, 2, 0, 3).reshape(local_tokens, head_count * HD)
    kv_cols = jnp.stack([grad_key, grad_value], 3).transpose(1, 2, 0, 3, 4)
    kv_cols = kv_cols.reshape(local_tokens, head_count * 2 * HD)
    weight_q = reduce_ctx(weight_term(activations, query_cols))
    weight_kv = lax.psum_scatter(weight_term(activations, kv_cols), "z", scatter_dimension=0, tiled=True)
    n_y = lax.psum(1, "y")
    width = activations.shape[1] // (2 * n_y)
    w_split = w_qkv.reshape(n_y, 2, width, w_qkv.shape[1])
    by_core = jnp.einsum("tk,ycwk->cytw", grad_qkv, w_split, preferred_element_type=f32)
    core_sum = ring_rs(by_core.astype(jnp.bfloat16), "c", 2)
    input_grad = ring_rs(core_sum, "y", n_y)
    input_grad, weight_q, weight_kv = lax.optimization_barrier((input_grad, weight_q, weight_kv))
    weight_kv = reduce_x(weight_kv)
    rows = weight_q.shape[0]
    weight_grad = jnp.concatenate(
        [weight_q.reshape(rows, head_count, 1, HD), weight_kv.reshape(rows, head_count, 2, HD)], 2
    ).reshape(rows, head_count * 3 * HD)
    return (from_blocks(attended), input_grad, weight_grad)


def solution(mesh):
    n_ctx, n_tp = mesh.devices.shape
    n_x = 4 if n_ctx % 4 == 0 else 1
    fine = Mesh(mesh.devices.reshape(n_ctx // n_x, n_x, n_tp // 2, 2), ("z", "x", "y", "c"))
    return jax.shard_map(
        per_device,
        mesh=fine,
        in_specs=(P(CTX, None), P(None, TP), P(TP, None), P(CTX, TP), P(CTX, TP)),
        out_specs=(P(CTX, TP), P(CTX, TP), P(CTX, TP)),
        check_vma=False,
    )
```
